32 devices in a mesh: groups: 2 (over x), seq: 16 (over z, y, core).
Axes of the slice: x: 2, y: 2, z: 4, core: 2. Of those that a mesh axis runs over, the one named last changes fastest.
Arguments:
- clean: bfloat16 [8192, 2048], P(('groups', 'seq')), parts along dimension 0, may hold values from -6 to 6
- delta: bfloat16 [8192, 2048], P(('groups', 'seq')), parts along dimension 0, may hold values from -0.25 to 0.25
- cotangent: bfloat16 [8192, 1024], P(('groups', 'seq')), parts along dimension 0, may hold values from -6 to 6
- w_query: bfloat16 [2048, 1024], P('seq'), may hold values from -0.125 to 0.125
- w_key: bfloat16 [2048, 1024], P('seq'), may hold values from -0.125 to 0.125
- w_value: bfloat16 [2048, 1024], P('seq'), may hold values from -0.125 to 0.125
- masks: int32 [32, 2, 2], P(('groups', 'seq')), parts along dimension 0, may hold values 0 or 1
Outputs:
- output: bfloat16 [8192, 1024], P(('groups', 'seq')), parts along dimension 0
- grad_input: bfloat16 [8192, 2048], P(('groups', 'seq')), parts along dimension 0
The draws below stay inside these ranges and needn't reach their ends.
There are 2 independent parts, one for each index of `groups`. The reference program is written for one: setup_inputs(seed, part) draws one part's arguments, and reference() takes and returns one part's arrays. A program takes and returns all parts, laid end to end along the dimension named above; an argument that names none is the same for every part. Nothing has to cross between parts.
All inputs are finite; a program needn't handle non-finite values. No bound on the sum of `masks` on one device may be relied on, other than what follows from the above.
Results may differ from the reference program's by a relative error of at most 0.012.
Values may be sent and summed in bfloat16 or wider, within the bound.
No kernel may reach another device: no remote copies, remote signals or barrier semaphores. Data moves between devices by JAX's collectives and lax.ppermute only.
A program may use at most 128 MiB of HBM per device.

```python
import jax
import jax.numpy as jnp
from jax import lax

D = 2048
NH = 8
DH = 128
BLK = 128
TOK_DEV = 256
HD = 1024
NB = 2
TOKENS = 4096
N_SEQ = 16


def place_ends(array, key, least, high):
    longest = array.shape.index(max(array.shape))
    spots = []
    for shift in (0, 1):
        where = [jax.random.randint(jax.random.fold_in(key, axis), (), 0, length) for axis, length in enumerate(array.shape)]
        where[longest] = (where[longest] + shift) % array.shape[longest]
        spots.append(tuple(where))
    return array.at[spots[0]].set(least).at[spots[1]].set(high)


def level_of(own_key, extent, pieces, least, top_value):
    def one(dim, shards_of):
        heights = jax.random.uniform(jax.random.fold_in(jax.random.fold_in(own_key, 6), dim), (shards_of,), jnp.float32, least / len(pieces), top_value / len(pieces))
        return jnp.repeat(jnp.exp(heights), extent[dim] // shards_of).reshape((-1,) + (1,) * (len(extent) - dim - 1))

    level = one(*pieces[0])
    for cut in pieces[1:]:
        level = level * one(*cut)
    return level


def normal_values(own_key, dims, scale, limit, split=(), held_as=jnp.bfloat16):
    factor_of = level_of(own_key, dims, split, -0.22, 0.18) if split else 1.0
    result = jax.random.normal(own_key, dims, jnp.float32) * scale * factor_of
    return jnp.minimum(jnp.maximum(result, -limit), limit).astype(held_as)


def setup_inputs(seed: int = 0, part: int = 0) -> dict:
    seeds = jax.random.split(jax.random.key(seed), 8)
    own_keys = jax.random.split(jax.random.fold_in(seeds[7], part), 8)
    return {
        "clean": normal_values(own_keys[0], (TOKENS, D), 1.0, 6.0, ((0, 16),)),
        "delta": jnp.clip(jax.random.uniform(own_keys[1], (TOKENS, D), jnp.float32, -0.25, 0.25) * level_of(own_keys[1], (TOKENS, D), ((0, 16),), -0.4, 0.0), -0.25, 0.25).astype(jnp.bfloat16),
        "cotangent": normal_values(own_keys[2], (TOKENS, HD), 1.0, 6.0, ((0, 16),)),
        "w_query": normal_values(seeds[3], (D, HD), D ** -0.5, 0.125, ((0, 16),)),
        "w_key": normal_values(seeds[4], (D, HD), D ** -0.5, 0.125, ((0, 16),)),
        "w_value": normal_values(seeds[5], (D, HD), D ** -0.5, 0.125, ((0, 16),)),
        "masks": place_ends((jax.random.randint(own_keys[6], (N_SEQ, NB, NB), 0, 4) < 3).astype(jnp.int32), jax.random.fold_in(own_keys[6], 1), 0, 1),
    }


EPSILON = 1e-06

def allowed_pairs(blocks, width):
    count = blocks.shape[0]
    row = jnp.arange(count)[:, None]
    col = jnp.arange(count)[None, :]
    inner_row = jnp.arange(width)[:, None]
    inner_col = jnp.arange(width)[None, :]
    lower = (row > col).astype(jnp.float32)[:, :, None, None]
    same = (row == col).astype(jnp.float32)[:, :, None, None] * (inner_row >= inner_col).astype(jnp.float32)[None, None]
    return blocks.astype(jnp.float32)[:, :, None, None] * (lower + same)

def forward_span(items):
    query, key, value, state, blocks, cotan = items
    allow = allowed_pairs(blocks, BLK)
    q32 = query.astype(jnp.float32)
    k32 = key.astype(jnp.float32)
    v32 = value.astype(jnp.float32)
    state_b = state.astype(jnp.bfloat16).astype(jnp.float32)
    scores = jnp.einsum('ibhd,jchd->hijbc', q32, k32)
    attn = (scores * allow).astype(jnp.bfloat16).astype(jnp.float32)
    mixed = jnp.einsum('hijbc,jchd->ibhd', attn, v32) + jnp.einsum('ibhd,hde->ibhe', q32, state_b)
    root = jnp.sqrt(lax.optimization_barrier(jnp.mean(mixed * mixed, axis=-1, keepdims=True)) + EPSILON)
    normed = mixed / root
    grad_out = cotan.astype(jnp.float32)
    d_mixed = (grad_out - normed * lax.optimization_barrier(jnp.mean(grad_out * normed, axis=-1, keepdims=True))) / root
    d_mixed_b = d_mixed.astype(jnp.bfloat16)
    grad_local = jnp.einsum('ibhd,ibhe->hde', q32, d_mixed_b.astype(jnp.float32))
    return (normed.astype(jnp.bfloat16), d_mixed_b, grad_local)

def backward_span(items):
    query, key, value, state, later, blocks, d_mixed_b = items
    allow = allowed_pairs(blocks, BLK)
    q32 = query.astype(jnp.float32)
    k32 = key.astype(jnp.float32)
    v32 = value.astype(jnp.float32)
    dm32 = d_mixed_b.astype(jnp.float32)
    state_b = state.astype(jnp.bfloat16).astype(jnp.float32)
    later_b = later.astype(jnp.bfloat16).astype(jnp.float32)
    scores = jnp.einsum('ibhd,jchd->hijbc', q32, k32)
    attn = (scores * allow).astype(jnp.bfloat16).astype(jnp.float32)
    d_attn = (jnp.einsum('ibhe,jche->hijbc', dm32, v32) * allow).astype(jnp.bfloat16).astype(jnp.float32)
    d_query = jnp.einsum('hijbc,jchd->ibhd', d_attn, k32) + jnp.einsum('ibhe,hde->ibhd', dm32, state_b)
    d_key = jnp.einsum('hijbc,ibhd->jchd', d_attn, q32) + jnp.einsum('jche,hde->jchd', v32, later_b)
    d_value = jnp.einsum('hijbc,ibhe->jche', attn, dm32) + jnp.einsum('jchd,hde->jche', k32, later_b)
    stacked = jnp.stack([d_query, d_key, d_value], axis=2).astype(jnp.bfloat16)
    return stacked.reshape(TOK_DEV, 3 * NH * DH)

def reference(clean, delta, cotangent, w_query, w_key, w_value, masks):
    x_in = (clean.astype(jnp.float32) + delta.astype(jnp.float32)).astype(jnp.bfloat16)
    w_cat = jnp.concatenate([w_query, w_key, w_value], axis=1)
    projected = jnp.dot(x_in, w_cat, preferred_element_type=jnp.float32).astype(jnp.bfloat16)
    spans = projected.reshape(N_SEQ, NB, BLK, 3, NH, DH)
    query = spans[:, :, :, 0]
    key = spans[:, :, :, 1]
    value = spans[:, :, :, 2]
    local = jnp.einsum('nibhd,nibhe->nhde', key.astype(jnp.float32), value.astype(jnp.float32))
    totals = jnp.cumsum(local, axis=0)
    prefix = jnp.concatenate([jnp.zeros_like(local[:1]), totals[:-1]], axis=0)
    cotan = cotangent.reshape(N_SEQ, NB, BLK, NH, DH)
    output, d_mixed_b, grad_local = lax.map(forward_span, (query, key, value, prefix, masks, cotan))
    rtotals = jnp.cumsum(grad_local[::-1], axis=0)[::-1]
    later = jnp.concatenate([rtotals[1:], jnp.zeros_like(grad_local[:1])], axis=0)
    d_proj = lax.map(backward_span, (query, key, value, prefix, later, masks, d_mixed_b))
    d_proj = d_proj.reshape(TOKENS, 3 * NH * DH)
    grad_input = lax.dot_general(d_proj, w_cat, (((1,), (1,)), ((), ())), preferred_element_type=jnp.float32)
    return (output.reshape(TOKENS, NH * DH), grad_input.astype(jnp.bfloat16))
```

```python
import jax
import jax.numpy as jnp
import numpy as np
from jax import lax
from jax.sharding import Mesh
from jax.sharding import PartitionSpec as P

DH = 128
BLK = 128

EPSILON = 1e-06

TOKENS = ("groups", "chip", "core")


def dense_allow(block_masks, tokens):
    blk = jnp.arange(tokens) // BLK
    gate = block_masks.astype(jnp.float32)[blk[:, None], blk[None, :]]
    causal = (jnp.arange(tokens)[None, :] <= jnp.arange(tokens)[:, None]).astype(jnp.float32)
    return gate * causal


def on_device(clean, delta, cotangent, w_query, w_key, w_value, masks):
    f32, bf16 = jnp.float32, jnp.bfloat16
    tok = clean.shape[0]
    feat = w_query.shape[1]
    half = feat // 2
    heads = half // DH
    k = lax.axis_index("core")
    c = lax.axis_index("chip")
    chips = lax.axis_size("chip")

    x_in = (clean.astype(f32) + delta.astype(f32)).astype(bf16)
    x_pair = lax.all_gather(x_in, "core", axis=0, tiled=True)

    def by_half(w):
        return w.reshape(w.shape[0], 2, half)

    w_loc = jnp.concatenate([by_half(w_query), by_half(w_key), by_half(w_value)], axis=2)
    w_loc = jnp.swapaxes(w_loc, 0, 1)
    w_chip = lax.all_to_all(w_loc, "core", 0, 0)
    w_chip = w_chip.reshape(-1, 3 * half)
    w_half = lax.all_gather(w_chip, "chip", axis=0, tiled=True)

    projected = jnp.dot(x_pair, w_half, preferred_element_type=f32).astype(bf16)
    projected = projected.reshape(2, tok, 3, heads, DH)
    query = projected[:, :, 0]
    key = projected[:, :, 1]
    value = projected[:, :, 2]

    local = jnp.einsum("jthd,jthe->jhde", key, value, preferred_element_type=f32)
    chip_total = local[0] + local[1]
    every = lax.all_gather(chip_total, "chip")
    before = (jnp.arange(chips) < c)[:, None, None, None]
    state0 = jnp.sum(jnp.where(before, every, 0.0), axis=0)
    state = jnp.stack([state0, state0 + local[0]])
    state_b = state.astype(bf16)

    pair_masks = lax.all_gather(masks[0], "core")
    allow = jax.vmap(dense_allow, in_axes=(0, None))(pair_masks, tok)

    scores = jnp.einsum("jthd,jshd->jhts", query, key, preferred_element_type=f32)
    attn = (scores * allow[:, None]).astype(bf16)
    mixed = jnp.einsum("jhts,jshd->jthd", attn, value, preferred_element_type=f32)
    mixed = mixed + jnp.einsum("jthd,jhde->jthe", query, state_b, preferred_element_type=f32)
    root = jnp.sqrt(jnp.mean(mixed * mixed, axis=-1, keepdims=True) + EPSILON)
    normed = mixed / root

    out_b = normed.astype(bf16).reshape(2, tok, half)
    out_b = lax.all_to_all(out_b, "core", 0, 0)
    output = jnp.swapaxes(out_b, 0, 1).reshape(tok, feat)

    cot = jnp.swapaxes(cotangent.reshape(tok, 2, half), 0, 1)
    cot = lax.all_to_all(cot, "core", 0, 0)
    grad_out = cot.astype(f32).reshape(2, tok, heads, DH)
    d_mixed = (grad_out - normed * jnp.mean(grad_out * normed, axis=-1, keepdims=True)) / root
    d_mixed_b = d_mixed.astype(bf16)
    grad_local = jnp.einsum("jthd,jthe->jhde", query, d_mixed_b, preferred_element_type=f32)

    grad_total = grad_local[0] + grad_local[1]
    every_g = lax.all_gather(grad_total, "chip")
    after = (jnp.arange(chips) > c)[:, None, None, None]
    later1 = jnp.sum(jnp.where(after, every_g, 0.0), axis=0)
    later = jnp.stack([later1 + grad_local[1], later1])
    later_b = later.astype(bf16)

    d_attn = (
        jnp.einsum("jthe,jshe->jhts", d_mixed_b, value, preferred_element_type=f32) * allow[:, None]
    ).astype(bf16)
    d_query = jnp.einsum("jhts,jshd->jthd", d_attn, key, preferred_element_type=f32)
    d_query = d_query + jnp.einsum("jthe,jhde->jthd", d_mixed_b, state_b, preferred_element_type=f32)
    d_key = jnp.einsum("jhts,jthd->jshd", d_attn, query, preferred_element_type=f32)
    d_key = d_key + jnp.einsum("jshe,jhde->jshd", value, later_b, preferred_element_type=f32)
    d_value = jnp.einsum("jhts,jthe->jshe", attn, d_mixed_b, preferred_element_type=f32)
    d_value = d_value + jnp.einsum("jshd,jhde->jshe", key, later_b, preferred_element_type=f32)
    d_proj = jnp.stack([d_query, d_key, d_value], axis=2).astype(bf16).reshape(2 * tok, 3 * half)

    partial = lax.dot_general(d_proj, w_half, (((1,), (1,)), ((), ())), preferred_element_type=f32)
    partial = partial.reshape(2, tok, -1)
    mine = jnp.where(k == 0, partial[0], partial[1])
    theirs = jnp.where(k == 0, partial[1], partial[0])
    received = lax.ppermute(theirs, "core", [(0, 1), (1, 0)])
    grad_input = (mine + received).astype(bf16)
    return (output, grad_input)


def solution(mesh):
    groups = mesh.shape["groups"]
    seq = mesh.shape["seq"]
    devices = np.asarray(mesh.devices).reshape(groups, seq // 2, 2)
    inner = Mesh(devices, TOKENS)
    rows = P(TOKENS, None)
    weights = P(("chip", "core"), None)
    return jax.shard_map(
        on_device,
        mesh=inner,
        in_specs=(rows, rows, rows, weights, weights, weights, P(TOKENS, None, None)),
        out_specs=(rows, rows),
        check_vma=False,
    )
```

```python
import jax
import jax.numpy as jnp
import numpy as np
from jax import lax
from jax.sharding import Mesh
from jax.sharding import PartitionSpec as P

DH = 128
BLK = 128

EPSILON = 1e-06

TOKENS = ("groups", "chip", "core")


def swap(x):
    return lax.ppermute(x, "core", [(0, 1), (1, 0)])


def ring_order(chips):
    if chips % 2:
        return list(range(chips))
    return list(range(0, chips, 2)) + list(range(chips - 1, 0, -2))


def ring_gather(block, chips, c):
    order = ring_order(chips)
    place = np.zeros(chips, np.int32)
    place[np.asarray(order)] = np.arange(chips)
    order_t = jnp.asarray(order, jnp.int32)
    here = jnp.asarray(place)[c]
    ahead = [(order[p], order[(p + 1) % chips]) for p in range(chips)]
    behind = [(order[p], order[(p - 1) % chips]) for p in range(chips)]
    got = [(c, block)]
    fwd = block
    bwd = block
    for step in range(1, chips // 2 + 1):
        fwd = lax.ppermute(fwd, "chip", ahead)
        got.append((order_t[(here - step) % chips], fwd))
        if step <= (chips - 1) // 2:
            bwd = lax.ppermute(bwd, "chip", behind)
            got.append((order_t[(here + step) % chips], bwd))
    return got


def exclusive_scan(total, chips, reverse):
    incl = total
    excl = jnp.zeros_like(total)
    d = 1
    while d < chips:
        if reverse:
            perm = [(i, i - d) for i in range(d, chips)]
        else:
            perm = [(i, i + d) for i in range(chips - d)]
        got = lax.ppermute(incl, "chip", perm)
        incl = incl + got
        excl = excl + got
        d *= 2
    return excl


def dense_allow(block_masks, tokens):
    nb = tokens // BLK
    gate = jnp.broadcast_to(
        block_masks.astype(jnp.float32)[:, None, :, None], (nb, BLK, nb, BLK)
    ).reshape(tokens, tokens)
    rows = lax.broadcasted_iota(jnp.int32, (tokens, tokens), 0)
    cols = lax.broadcasted_iota(jnp.int32, (tokens, tokens), 1)
    return jnp.where(cols <= rows, gate, 0.0)


def on_device(clean, delta, cotangent, w_query, w_key, w_value, masks):
    f32, bf16 = jnp.float32, jnp.bfloat16
    tok = clean.shape[0]
    feat = w_query.shape[1]
    half = feat // 2
    heads = half // DH
    rows_dev = w_query.shape[0]
    k = lax.axis_index("core")
    c = lax.axis_index("chip")
    chips = lax.axis_size("chip")
    first = k == 0

    x_in = (clean.astype(f32) + delta.astype(f32)).astype(bf16)
    x_pair = jnp.concatenate([x_in, swap(x_in)], axis=0)

    w_cat = jnp.concatenate(
        [w.reshape(rows_dev, 2, half) for w in (w_query, w_key, w_value)], axis=2
    )
    w_mine = jnp.where(first, w_cat[:, 0], w_cat[:, 1])
    w_other = jnp.where(first, w_cat[:, 1], w_cat[:, 0])
    w_recv = swap(w_other)
    chip_rows = jnp.where(
        first,
        jnp.concatenate([w_mine, w_recv], axis=0),
        jnp.concatenate([w_recv, w_mine], axis=0),
    )
    pieces = ring_gather(chip_rows, chips, c)

    span = 2 * rows_dev
    projected = None
    w_half = jnp.zeros((chips * span, 3 * half), bf16)
    for src, piece in pieces:
        x_cols = lax.dynamic_slice_in_dim(x_pair, src * span, span, axis=1)
        term = jnp.dot(x_cols, piece, preferred_element_type=f32)
        projected = term if projected is None else projected + term
        w_half = lax.dynamic_update_slice_in_dim(w_half, piece, src * span, axis=0)
    projected = projected.astype(bf16).reshape(2, tok, 3, heads, DH)
    query = projected[:, :, 0]
    key = projected[:, :, 1]
    value = projected[:, :, 2]

    local = jnp.einsum("jthd,jthe->jhde", key, value, preferred_element_type=f32)
    state0 = exclusive_scan(local[0] + local[1], chips, False)
    state_mine = jnp.where(first, state0, state0 + local[1])
    state_other = jnp.where(first, state0 + local[0], state0)
    state_b = jnp.stack([state_mine, state_other]).astype(bf16)

    pair_masks = jnp.stack([masks[0], swap(masks[0])])
    allow = jax.vmap(dense_allow, in_axes=(0, None))(pair_masks, tok)

    scores = jnp.einsum("jthd,jshd->jhts", query, key, preferred_element_type=f32)
    attn = (scores * allow[:, None]).astype(bf16)
    mixed = jnp.einsum("jhts,jshd->jthd", attn, value, preferred_element_type=f32)
    mixed = mixed + jnp.einsum("jthd,jhde->jthe", query, state_b, preferred_element_type=f32)
    root = jnp.sqrt(jnp.mean(mixed * mixed, axis=-1, keepdims=True) + EPSILON)
    normed = mixed / root

    out_b = normed.astype(bf16).reshape(2, tok, half)
    out_recv = swap(out_b[1])
    output = jnp.where(
        first,
        jnp.concatenate([out_b[0], out_recv], axis=1),
        jnp.concatenate([out_recv, out_b[0]], axis=1),
    )

    cot = cotangent.reshape(tok, 2, half)
    cot_mine = jnp.where(first, cot[:, 0], cot[:, 1])
    cot_other = jnp.where(first, cot[:, 1], cot[:, 0])
    grad_out = jnp.stack([cot_mine, swap(cot_other)]).astype(f32).reshape(2, tok, heads, DH)
    d_mixed = (grad_out - normed * jnp.mean(grad_out * normed, axis=-1, keepdims=True)) / root
    d_mixed_b = d_mixed.astype(bf16)
    grad_local = jnp.einsum("jthd,jthe->jhde", query, d_mixed_b, preferred_element_type=f32)

    later1 = exclusive_scan(grad_local[0] + grad_local[1], chips, True)
    later_mine = jnp.where(first, later1 + grad_local[1], later1)
    later_other = jnp.where(first, later1, later1 + grad_local[0])
    later_b = jnp.stack([later_mine, later_other]).astype(bf16)

    d_attn = (
        jnp.einsum("jthe,jshe->jhts", d_mixed_b, value, preferred_element_type=f32) * allow[:, None]
    ).astype(bf16)
    d_query = jnp.einsum("jhts,jshd->jthd", d_attn, key, preferred_element_type=f32)
    d_query = d_query + jnp.einsum("jthe,jhde->jthd", d_mixed_b, state_b, preferred_element_type=f32)
    d_key = jnp.einsum("jhts,jthd->jshd", d_attn, query, preferred_element_type=f32)
    d_key = d_key + jnp.einsum("jshe,jhde->jshd", value, later_b, preferred_element_type=f32)
    d_value = jnp.einsum("jhts,jthe->jshe", attn, d_mixed_b, preferred_element_type=f32)
    d_value = d_value + jnp.einsum("jshd,jhde->jshe", key, later_b, preferred_element_type=f32)
    d_proj = jnp.stack([d_query, d_key, d_value], axis=2).astype(bf16).reshape(2 * tok, 3 * half)

    partial = lax.dot_general(d_proj, w_half, (((1,), (1,)), ((), ())), preferred_element_type=f32)
    partial = partial.reshape(2, tok, -1)
    grad_input = (partial[0] + swap(partial[1])).astype(bf16)
    return (output, grad_input)


def solution(mesh):
    groups = mesh.shape["groups"]
    seq = mesh.shape["seq"]
    devices = np.asarray(mesh.devices).reshape(groups, seq // 2, 2)
    inner = Mesh(devices, TOKENS)
    rows = P(TOKENS, None)
    weights = P(("chip", "core"), None)
    return jax.shard_map(
        on_device,
        mesh=inner,
        in_specs=(rows, rows, rows, weights, weights, weights, P(TOKENS, None, None)),
        out_specs=(rows, rows),
        check_vma=False,
    )
```

```python
import jax
import jax.numpy as jnp
import numpy as np
from jax import lax
from jax.sharding import Mesh
from jax.sharding import PartitionSpec as P

DH = 128
BLK = 128

EPSILON = 1e-06

TOKENS = ("groups", "chip", "core")


def swap(x):
    return lax.ppermute(x, "core", [(0, 1), (1, 0)])


def ring_order(chips):
    if chips % 2:
        return list(range(chips))
    return list(range(0, chips, 2)) + list(range(chips - 1, 0, -2))


def ring_gather(block, chips, c):
    order = ring_order(chips)
    place = np.zeros(chips, np.int32)
    place[np.asarray(order)] = np.arange(chips)
    order_t = jnp.asarray(order, jnp.int32)
    here = jnp.asarray(place)[c]
    ahead = [(order[p], order[(p + 1) % chips]) for p in range(chips)]
    behind = [(order[p], order[(p - 1) % chips]) for p in range(chips)]
    got = [(c, block)]
    fwd = block
    bwd = block
    for step in range(1, chips // 2 + 1):
        fwd = lax.ppermute(fwd, "chip", ahead)
        got.append((order_t[(here - step) % chips], fwd))
        if step <= (chips - 1) // 2:
            bwd = lax.ppermute(bwd, "chip", behind)
            got.append((order_t[(here + step) % chips], bwd))
    return got


def exclusive_scan(total, chips, reverse):
    incl = total
    excl = jnp.zeros_like(total)
    d = 1
    while d < chips:
        if reverse:
            perm = [(i, i - d) for i in range(d, chips)]
        else:
            perm = [(i, i + d) for i in range(chips - d)]
        got = lax.ppermute(incl, "chip", perm)
        incl = incl + got
        excl = excl + got
        d *= 2
    return excl


def dense_allow(block_masks, tokens):
    nb = tokens // BLK
    gate = jnp.broadcast_to(
        block_masks.astype(jnp.float32)[:, None, :, None], (nb, BLK, nb, BLK)
    ).reshape(tokens, tokens)
    rows = lax.broadcasted_iota(jnp.int32, (tokens, tokens), 0)
    cols = lax.broadcasted_iota(jnp.int32, (tokens, tokens), 1)
    return jnp.where(cols <= rows, gate, 0.0)


def on_device(clean, delta, cotangent, w_query, w_key, w_value, masks):
    f32, bf16 = jnp.float32, jnp.bfloat16
    tok = clean.shape[0]
    feat = w_query.shape[1]
    half = feat // 2
    heads = half // DH
    rows_dev = w_query.shape[0]
    k = lax.axis_index("core")
    c = lax.axis_index("chip")
    chips = lax.axis_size("chip")
    first = k == 0

    x_in = (clean.astype(f32) + delta.astype(f32)).astype(bf16)
    x_pair = jnp.concatenate([x_in, swap(x_in)], axis=0)

    def cols(w, which):
        return lax.dynamic_slice_in_dim(w, which * half, half, axis=1)

    def chip_block(mats):
        mine = jnp.concatenate([cols(w, k) for w in mats], axis=1)
        recv = swap(jnp.concatenate([cols(w, 1 - k) for w in mats], axis=1))
        block = jnp.zeros((2 * rows_dev, mine.shape[1]), mine.dtype)
        block = lax.dynamic_update_slice_in_dim(block, mine, k * rows_dev, axis=0)
        return lax.dynamic_update_slice_in_dim(block, recv, (1 - k) * rows_dev, axis=0)

    span = 2 * rows_dev

    def project(pieces):
        out = None
        full = jnp.zeros((chips * span, pieces[0][1].shape[1]), bf16)
        for src, piece in pieces:
            x_cols = lax.dynamic_slice_in_dim(x_pair, src * span, span, axis=1)
            term = jnp.dot(x_cols, piece, preferred_element_type=f32)
            out = term if out is None else out + term
            full = lax.dynamic_update_slice_in_dim(full, piece, src * span, axis=0)
        return out.astype(bf16), full

    kv_pieces = ring_gather(chip_block((w_key, w_value)), chips, c)
    q_block, _ = lax.optimization_barrier((chip_block((w_query,)), kv_pieces[-1][1]))
    q_pieces = ring_gather(q_block, chips, c)
    kv_proj, w_kv = project(kv_pieces)
    q_proj, w_q = project(q_pieces)
    kv_proj = kv_proj.reshape(2, tok, 2, heads, DH)
    query = q_proj.reshape(2, tok, heads, DH)
    key = kv_proj[:, :, 0]
    value = kv_proj[:, :, 1]

    local = jnp.einsum("jthd,jthe->jhde", key, value, preferred_element_type=f32)
    state0 = exclusive_scan(local[0] + local[1], chips, False)
    state_mine = jnp.where(first, state0, state0 + local[1])
    state_other = jnp.where(first, state0 + local[0], state0)
    state_b = jnp.stack([state_mine, state_other]).astype(bf16)

    pair_masks = jnp.stack([masks[0], swap(masks[0])])
    allow = jax.vmap(dense_allow, in_axes=(0, None))(pair_masks, tok)

    scores = jnp.einsum("jthd,jshd->jhts", query, key, preferred_element_type=f32)
    attn = (scores * allow[:, None]).astype(bf16)
    mixed = jnp.einsum("jhts,jshd->jthd", attn, value, preferred_element_type=f32)
    mixed = mixed + jnp.einsum("jthd,jhde->jthe", query, state_b, preferred_element_type=f32)
    root = jnp.sqrt(jnp.mean(mixed * mixed, axis=-1, keepdims=True) + EPSILON)
    normed = mixed / root

    out_b = normed.astype(bf16).reshape(2, tok, half)
    out_recv = swap(out_b[1])
    output = jnp.where(
        first,
        jnp.concatenate([out_b[0], out_recv], axis=1),
        jnp.concatenate([out_recv, out_b[0]], axis=1),
    )

    cot = cotangent.reshape(tok, 2, half)
    cot_mine = jnp.where(first, cot[:, 0], cot[:, 1])
    cot_other = jnp.where(first, cot[:, 1], cot[:, 0])
    grad_out = jnp.stack([cot_mine, swap(cot_other)]).astype(f32).reshape(2, tok, heads, DH)
    d_mixed = (grad_out - normed * jnp.mean(grad_out * normed, axis=-1, keepdims=True)) / root
    d_mixed_b = d_mixed.astype(bf16)
    grad_local = jnp.einsum("jthd,jthe->jhde", query, d_mixed_b, preferred_element_type=f32)

    later1 = exclusive_scan(grad_local[0] + grad_local[1], chips, True)
    later_mine = jnp.where(first, later1 + grad_local[1], later1)
    later_other = jnp.where(first, later1, later1 + grad_local[0])
    later_b = jnp.stack([later_mine, later_other]).astype(bf16)

    d_attn = (
        jnp.einsum("jthe,jshe->jhts", d_mixed_b, value, preferred_element_type=f32) * allow[:, None]
    ).astype(bf16)
    d_query = jnp.einsum("jhts,jshd->jthd", d_attn, key, preferred_element_type=f32)
    d_query = d_query + jnp.einsum("jthe,jhde->jthd", d_mixed_b, state_b, preferred_element_type=f32)
    d_key = jnp.einsum("jhts,jthd->jshd", d_attn, query, preferred_element_type=f32)
    d_key = d_key + jnp.einsum("jshe,jhde->jshd", value, later_b, preferred_element_type=f32)
    d_value = jnp.einsum("jhts,jthe->jshe", attn, d_mixed_b, preferred_element_type=f32)
    d_value = d_value + jnp.einsum("jshd,jhde->jshe", key, later_b, preferred_element_type=f32)
    dq_b = d_query.astype(bf16).reshape(2, tok, half)
    dkv_b = jnp.stack([d_key, d_value], axis=2).astype(bf16).reshape(2, tok, 2 * half)

    def grad_rows(j):
        g = lax.dot_general(dq_b[j], w_q, (((1,), (1,)), ((), ())), preferred_element_type=f32)
        return g + lax.dot_general(dkv_b[j], w_kv, (((1,), (1,)), ((), ())), preferred_element_type=f32)

    received = swap(grad_rows(1))
    grad_input = (grad_rows(0) + received).astype(bf16)
    return (output, grad_input)


def solution(mesh):
    groups = mesh.shape["groups"]
    seq = mesh.shape["seq"]
    devices = np.asarray(mesh.devices).reshape(groups, seq // 2, 2)
    inner = Mesh(devices, TOKENS)
    rows = P(TOKENS, None)
    weights = P(("chip", "core"), None)
    return jax.shard_map(
        on_device,
        mesh=inner,
        in_specs=(rows, rows, rows, weights, weights, weights, P(TOKENS, None, None)),
        out_specs=(rows, rows),
        check_vma=False,
    )
```

```python
import jax
import jax.numpy as jnp
import numpy as np
from jax import lax
from jax.sharding import Mesh
from jax.sharding import PartitionSpec as P

DH = 128
BLK = 128

EPSILON = 1e-06

TOKENS = ("groups", "chip", "core")


def swap(x):
    return lax.ppermute(x, "core", [(0, 1), (1, 0)])


def ring_order(chips):
    if chips % 2:
        return list(range(chips))
    return list(range(0, chips, 2)) + list(range(chips - 1, 0, -2))


def ring_gather(block, chips, c, p):
    order = ring_order(chips)
    place = np.zeros(chips, np.int32)
    place[np.asarray(order)] = np.arange(chips)
    order_t = jnp.asarray(order, jnp.int32)
    here = jnp.asarray(place)[c]
    ahead = [(order[p_], order[(p_ + 1) % chips]) for p_ in range(chips)]
    behind = [(order[p_], order[(p_ - 1) % chips]) for p_ in range(chips)]
    share = block.shape[1] // 3
    width = block.shape[1] - share
    groups = lax.axis_size("groups")
    partner = [(g, g ^ 1) for g in range(groups)]

    def land(piece):
        sent = lax.dynamic_slice_in_dim(piece, p * share, share, axis=1)
        other = lax.ppermute(sent, "groups", partner)
        return [(piece, p * share), (other, (1 - p) * width)]

    got = [(c, [(block, 0)])]
    fwd = lax.dynamic_slice_in_dim(block, p * share, width, axis=1)
    bwd = fwd
    for step in range(1, chips // 2 + 1):
        fwd = lax.ppermute(fwd, "chip", ahead)
        got.append((order_t[(here - step) % chips], land(fwd)))
        if step <= (chips - 1) // 2:
            bwd = lax.ppermute(bwd, "chip", behind)
            got.append((order_t[(here + step) % chips], land(bwd)))
    return got


def exclusive_scan(total, chips, reverse):
    incl = total
    excl = jnp.zeros_like(total)
    d = 1
    while d < chips:
        if reverse:
            perm = [(i, i - d) for i in range(d, chips)]
        else:
            perm = [(i, i + d) for i in range(chips - d)]
        got = lax.ppermute(incl, "chip", perm)
        incl = incl + got
        excl = excl + got
        d *= 2
    return excl


def dense_allow(block_masks, tokens):
    nb = tokens // BLK
    gate = jnp.broadcast_to(
        block_masks.astype(jnp.float32)[:, None, :, None], (nb, BLK, nb, BLK)
    ).reshape(tokens, tokens)
    rows = lax.broadcasted_iota(jnp.int32, (tokens, tokens), 0)
    cols = lax.broadcasted_iota(jnp.int32, (tokens, tokens), 1)
    return jnp.where(cols <= rows, gate, 0.0)


def on_device(clean, delta, cotangent, w_query, w_key, w_value, masks):
    f32, bf16 = jnp.float32, jnp.bfloat16
    tok = clean.shape[0]
    feat = w_query.shape[1]
    half = feat // 2
    heads = half // DH
    rows_dev = w_query.shape[0]
    k = lax.axis_index("core")
    c = lax.axis_index("chip")
    chips = lax.axis_size("chip")
    first = k == 0

    x_in = (clean.astype(f32) + delta.astype(f32)).astype(bf16)
    x_pair = jnp.concatenate([x_in, swap(x_in)], axis=0)

    def cols(w, which):
        return lax.dynamic_slice_in_dim(w, which * half, half, axis=1)

    def chip_block(mats):
        mine = jnp.concatenate([cols(w, k) for w in mats], axis=1)
        recv = swap(jnp.concatenate([cols(w, 1 - k) for w in mats], axis=1))
        block = jnp.zeros((2 * rows_dev, mine.shape[1]), mine.dtype)
        block = lax.dynamic_update_slice_in_dim(block, mine, k * rows_dev, axis=0)
        return lax.dynamic_update_slice_in_dim(block, recv, (1 - k) * rows_dev, axis=0)

    span = 2 * rows_dev
    block = chip_block((w_query, w_key, w_value))
    w_half = jnp.zeros((chips * span, block.shape[1]), bf16)
    for src, parts in ring_gather(block, chips, c, lax.axis_index("groups") % 2):
        for piece, col in parts:
            w_half = lax.dynamic_update_slice(w_half, piece, (src * span, col))
    projected = jnp.dot(x_pair, w_half, preferred_element_type=f32).astype(bf16)
    projected = projected.reshape(2, tok, 3, heads, DH)
    query = projected[:, :, 0]
    key = projected[:, :, 1]
    value = projected[:, :, 2]

    local = jnp.einsum("jthd,jthe->jhde", key, value, preferred_element_type=f32)
    state0 = exclusive_scan(local[0] + local[1], chips, False)
    state_mine = jnp.where(first, state0, state0 + local[1])
    state_other = jnp.where(first, state0 + local[0], state0)
    state_b = jnp.stack([state_mine, state_other]).astype(bf16)

    pair_masks = jnp.stack([masks[0], swap(masks[0])])
    allow = jax.vmap(dense_allow, in_axes=(0, None))(pair_masks, tok)

    scores = jnp.einsum("jthd,jshd->jhts", query, key, preferred_element_type=f32)
    attn = (scores * allow[:, None]).astype(bf16)
    mixed = jnp.einsum("jhts,jshd->jthd", attn, value, preferred_element_type=f32)
    mixed = mixed + jnp.einsum("jthd,jhde->jthe", query, state_b, preferred_element_type=f32)
    root = jnp.sqrt(jnp.mean(mixed * mixed, axis=-1, keepdims=True) + EPSILON)
    normed = mixed / root

    out_b = normed.astype(bf16).reshape(2, tok, half)
    out_recv = swap(out_b[1])
    output = jnp.where(
        first,
        jnp.concatenate([out_b[0], out_recv], axis=1),
        jnp.concatenate([out_recv, out_b[0]], axis=1),
    )

    cot = cotangent.reshape(tok, 2, half)
    cot_mine = jnp.where(first, cot[:, 0], cot[:, 1])
    cot_other = jnp.where(first, cot[:, 1], cot[:, 0])
    grad_out = jnp.stack([cot_mine, swap(cot_other)]).astype(f32).reshape(2, tok, heads, DH)
    d_mixed = (grad_out - normed * jnp.mean(grad_out * normed, axis=-1, keepdims=True)) / root
    d_mixed_b = d_mixed.astype(bf16)
    grad_local = jnp.einsum("jthd,jthe->jhde", query, d_mixed_b, preferred_element_type=f32)

    later1 = exclusive_scan(grad_local[0] + grad_local[1], chips, True)
    later_mine = jnp.where(first, later1 + grad_local[1], later1)
    later_other = jnp.where(first, later1, later1 + grad_local[0])
    later_b = jnp.stack([later_mine, later_other]).astype(bf16)

    d_attn = (
        jnp.einsum("jthe,jshe->jhts", d_mixed_b, value, preferred_element_type=f32) * allow[:, None]
    ).astype(bf16)
    d_query = jnp.einsum("jhts,jshd->jthd", d_attn, key, preferred_element_type=f32)
    d_query = d_query + jnp.einsum("jthe,jhde->jthd", d_mixed_b, state_b, preferred_element_type=f32)
    d_key = jnp.einsum("jhts,jthd->jshd", d_attn, query, preferred_element_type=f32)
    d_key = d_key + jnp.einsum("jshe,jhde->jshd", value, later_b, preferred_element_type=f32)
    d_value = jnp.einsum("jhts,jthe->jshe", attn, d_mixed_b, preferred_element_type=f32)
    d_value = d_value + jnp.einsum("jshd,jhde->jshe", key, later_b, preferred_element_type=f32)
    d_proj = jnp.stack([d_query, d_key, d_value], axis=2).astype(bf16).reshape(2, tok, 3 * half)

    def grad_rows(j):
        return lax.dot_general(d_proj[j], w_half, (((1,), (1,)), ((), ())), preferred_element_type=f32)

    received = swap(grad_rows(1))
    grad_input = (grad_rows(0) + received).astype(bf16)
    return (output, grad_input)


def solution(mesh):
    groups = mesh.shape["groups"]
    seq = mesh.shape["seq"]
    devices = np.asarray(mesh.devices).reshape(groups, seq // 2, 2)
    inner = Mesh(devices, TOKENS)
    rows = P(TOKENS, None)
    weights = P(("chip", "core"), None)
    return jax.shard_map(
        on_device,
        mesh=inner,
        in_specs=(rows, rows, rows, weights, weights, weights, P(TOKENS, None, None)),
        out_specs=(rows, rows),
        check_vma=False,
    )
```

```python
import jax
import jax.numpy as jnp
import numpy as np
from jax import lax
from jax.sharding import Mesh
from jax.sharding import PartitionSpec as P

DH = 128
BLK = 128

EPSILON = 1e-06

TOKENS = ("groups", "chip", "core")


def swap(x):
    return lax.ppermute(x, "core", [(0, 1), (1, 0)])


def ring_order(chips):
    if chips % 2:
        return list(range(chips))
    return list(range(0, chips, 2)) + list(range(chips - 1, 0, -2))


def ring_gather(block, chips, c, p):
    order = ring_order(chips)
    place = np.zeros(chips, np.int32)
    place[np.asarray(order)] = np.arange(chips)
    order_t = jnp.asarray(order, jnp.int32)
    here = jnp.asarray(place)[c]
    ahead = [(order[p_], order[(p_ + 1) % chips]) for p_ in range(chips)]
    behind = [(order[p_], order[(p_ - 1) % chips]) for p_ in range(chips)]
    share = block.shape[1] // 3
    width = block.shape[1] - share
    groups = lax.axis_size("groups")
    partner = [(g, g ^ 1) for g in range(groups)]

    def land(piece):
        sent = lax.dynamic_slice_in_dim(piece, p * share, share, axis=1)
        return (piece, lax.ppermute(sent, "groups", partner))

    fwd = lax.dynamic_slice_in_dim(block, p * share, width, axis=1)
    got = [(c, (fwd, lax.dynamic_slice_in_dim(block, (1 - p) * width, share, axis=1)))]
    bwd = fwd
    for step in range(1, chips // 2 + 1):
        fwd = lax.ppermute(fwd, "chip", ahead)
        got.append((order_t[(here - step) % chips], land(fwd)))
        if step <= (chips - 1) // 2:
            bwd = lax.ppermute(bwd, "chip", behind)
            got.append((order_t[(here + step) % chips], land(bwd)))
    return got


def exclusive_scan(total, chips, reverse):
    incl = total
    excl = jnp.zeros_like(total)
    d = 1
    while d < chips:
        if reverse:
            perm = [(i, i - d) for i in range(d, chips)]
        else:
            perm = [(i, i + d) for i in range(chips - d)]
        got = lax.ppermute(incl, "chip", perm)
        incl = incl + got
        excl = excl + got
        d *= 2
    return excl


def dense_allow(block_masks, tokens):
    nb = tokens // BLK
    gate = jnp.broadcast_to(
        block_masks.astype(jnp.float32)[:, None, :, None], (nb, BLK, nb, BLK)
    ).reshape(tokens, tokens)
    rows = lax.broadcasted_iota(jnp.int32, (tokens, tokens), 0)
    cols = lax.broadcasted_iota(jnp.int32, (tokens, tokens), 1)
    return jnp.where(cols <= rows, gate, 0.0)


def on_device(clean, delta, cotangent, w_query, w_key, w_value, masks):
    f32, bf16 = jnp.float32, jnp.bfloat16
    tok = clean.shape[0]
    feat = w_query.shape[1]
    half = feat // 2
    heads = half // DH
    rows_dev = w_query.shape[0]
    k = lax.axis_index("core")
    c = lax.axis_index("chip")
    chips = lax.axis_size("chip")
    first = k == 0

    x_in = (clean.astype(f32) + delta.astype(f32)).astype(bf16)
    x_pair = jnp.concatenate([x_in, swap(x_in)], axis=0)

    def cols(w, which):
        return lax.dynamic_slice_in_dim(w, which * half, half, axis=1)

    def chip_block(mats):
        mine = jnp.concatenate([cols(w, k) for w in mats], axis=1)
        recv = swap(jnp.concatenate([cols(w, 1 - k) for w in mats], axis=1))
        block = jnp.zeros((2 * rows_dev, mine.shape[1]), mine.dtype)
        block = lax.dynamic_update_slice_in_dim(block, mine, k * rows_dev, axis=0)
        return lax.dynamic_update_slice_in_dim(block, recv, (1 - k) * rows_dev, axis=0)

    span = 2 * rows_dev
    block = chip_block((w_query, w_key, w_value))
    parity = lax.axis_index("groups") % 2
    share = half
    width = 2 * half
    w_ring = jnp.zeros((chips * span, width), bf16)
    w_x = jnp.zeros((chips * span, share), bf16)
    for src, (ringed, swapped) in ring_gather(block, chips, c, parity):
        w_ring = lax.dynamic_update_slice_in_dim(w_ring, ringed, src * span, axis=0)
        w_x = lax.dynamic_update_slice_in_dim(w_x, swapped, src * span, axis=0)
    p_ring = jnp.dot(x_pair, w_ring, preferred_element_type=f32).astype(bf16)
    p_x = jnp.dot(x_pair, w_x, preferred_element_type=f32).astype(bf16)
    projected = jnp.where(
        parity == 0,
        jnp.concatenate([p_ring, p_x], axis=1),
        jnp.concatenate([p_x, p_ring], axis=1),
    )
    projected = projected.reshape(2, tok, 3, heads, DH)
    query = projected[:, :, 0]
    key = projected[:, :, 1]
    value = projected[:, :, 2]

    local = jnp.einsum("jthd,jthe->jhde", key, value, preferred_element_type=f32)
    state0 = exclusive_scan(local[0] + local[1], chips, False)
    state_mine = jnp.where(first, state0, state0 + local[1])
    state_other = jnp.where(first, state0 + local[0], state0)
    state_b = jnp.stack([state_mine, state_other]).astype(bf16)

    pair_masks = jnp.stack([masks[0], swap(masks[0])])
    allow = jax.vmap(dense_allow, in_axes=(0, None))(pair_masks, tok)

    scores = jnp.einsum("jthd,jshd->jhts", query, key, preferred_element_type=f32)
    attn = (scores * allow[:, None]).astype(bf16)
    mixed = jnp.einsum("jhts,jshd->jthd", attn, value, preferred_element_type=f32)
    mixed = mixed + jnp.einsum("jthd,jhde->jthe", query, state_b, preferred_element_type=f32)
    root = jnp.sqrt(jnp.mean(mixed * mixed, axis=-1, keepdims=True) + EPSILON)
    normed = mixed / root

    out_b = normed.astype(bf16).reshape(2, tok, half)
    out_recv = swap(out_b[1])
    output = jnp.where(
        first,
        jnp.concatenate([out_b[0], out_recv], axis=1),
        jnp.concatenate([out_recv, out_b[0]], axis=1),
    )

    cot = cotangent.reshape(tok, 2, half)
    cot_mine = jnp.where(first, cot[:, 0], cot[:, 1])
    cot_other = jnp.where(first, cot[:, 1], cot[:, 0])
    grad_out = jnp.stack([cot_mine, swap(cot_other)]).astype(f32).reshape(2, tok, heads, DH)
    d_mixed = (grad_out - normed * jnp.mean(grad_out * normed, axis=-1, keepdims=True)) / root
    d_mixed_b = d_mixed.astype(bf16)
    grad_local = jnp.einsum("jthd,jthe->jhde", query, d_mixed_b, preferred_element_type=f32)

    later1 = exclusive_scan(grad_local[0] + grad_local[1], chips, True)
    later_mine = jnp.where(first, later1 + grad_local[1], later1)
    later_other = jnp.where(first, later1, later1 + grad_local[0])
    later_b = jnp.stack([later_mine, later_other]).astype(bf16)

    d_attn = (
        jnp.einsum("jthe,jshe->jhts", d_mixed_b, value, preferred_element_type=f32) * allow[:, None]
    ).astype(bf16)
    d_query = jnp.einsum("jhts,jshd->jthd", d_attn, key, preferred_element_type=f32)
    d_query = d_query + jnp.einsum("jthe,jhde->jthd", d_mixed_b, state_b, preferred_element_type=f32)
    d_key = jnp.einsum("jhts,jthd->jshd", d_attn, query, preferred_element_type=f32)
    d_key = d_key + jnp.einsum("jshe,jhde->jshd", value, later_b, preferred_element_type=f32)
    d_value = jnp.einsum("jhts,jthe->jshe", attn, d_mixed_b, preferred_element_type=f32)
    d_value = d_value + jnp.einsum("jshd,jhde->jshe", key, later_b, preferred_element_type=f32)
    d_proj = jnp.stack([d_query, d_key, d_value], axis=2).astype(bf16).reshape(2, tok, 3 * half)

    def grad_rows(j):
        d_ring = lax.dynamic_slice_in_dim(d_proj[j], parity * share, width, axis=1)
        d_x = lax.dynamic_slice_in_dim(d_proj[j], (1 - parity) * width, share, axis=1)
        g = lax.dot_general(d_ring, w_ring, (((1,), (1,)), ((), ())), preferred_element_type=f32)
        return g + lax.dot_general(d_x, w_x, (((1,), (1,)), ((), ())), preferred_element_type=f32)

    received = swap(grad_rows(1))
    grad_input = (grad_rows(0) + received).astype(bf16)
    return (output, grad_input)


def solution(mesh):
    groups = mesh.shape["groups"]
    seq = mesh.shape["seq"]
    devices = np.asarray(mesh.devices).reshape(groups, seq // 2, 2)
    inner = Mesh(devices, TOKENS)
    rows = P(TOKENS, None)
    weights = P(("chip", "core"), None)
    return jax.shard_map(
        on_device,
        mesh=inner,
        in_specs=(rows, rows, rows, weights, weights, weights, P(TOKENS, None, None)),
        out_specs=(rows, rows),
        check_vma=False,
    )
```

```python
import jax
import jax.numpy as jnp
import numpy as np
from jax import lax
from jax.sharding import Mesh
from jax.sharding import PartitionSpec as P

DH = 128
BLK = 128

EPSILON = 1e-06

TOKENS = ("groups", "chip", "core")


def swap(x):
    return lax.ppermute(x, "core", [(0, 1), (1, 0)])


def ring_order(chips):
    if chips % 2:
        return list(range(chips))
    return list(range(0, chips, 2)) + list(range(chips - 1, 0, -2))


def ring_gather(block, chips, c, p):
    order = ring_order(chips)
    place = np.zeros(chips, np.int32)
    place[np.asarray(order)] = np.arange(chips)
    order_t = jnp.asarray(order, jnp.int32)
    here = jnp.asarray(place)[c]
    ahead = [(order[i], order[(i + 1) % chips]) for i in range(chips)]
    behind = [(order[i], order[(i - 1) % chips]) for i in range(chips)]
    span = block.shape[0]
    share = (span * 3 // 8) // 8 * 8
    width = span - share
    groups = lax.axis_size("groups")
    partner = [(g, g ^ 1) for g in range(groups)]

    def land(src, piece):
        sent = lax.dynamic_slice_in_dim(piece, p * (width - share), share, axis=0)
        other = lax.ppermute(sent, "groups", partner)
        return [(src, p * share, piece), (src, (1 - p) * width, other)]

    fwd = lax.dynamic_slice_in_dim(block, p * share, width, axis=0)
    bwd = fwd
    got = [(c, 0, block)]
    for step in range(1, chips // 2 + 1):
        fwd = lax.ppermute(fwd, "chip", ahead)
        got += land(order_t[(here - step) % chips], fwd)
        if step <= (chips - 1) // 2:
            bwd = lax.ppermute(bwd, "chip", behind)
            got += land(order_t[(here + step) % chips], bwd)
    return got


def exclusive_scan(total, chips, reverse):
    incl = total
    excl = jnp.zeros_like(total)
    d = 1
    while d < chips:
        if reverse:
            perm = [(i, i - d) for i in range(d, chips)]
        else:
            perm = [(i, i + d) for i in range(chips - d)]
        got = lax.ppermute(incl, "chip", perm)
        incl = incl + got
        excl = excl + got
        d *= 2
    return excl


def dense_allow(block_masks, tokens):
    nb = tokens // BLK
    gate = jnp.broadcast_to(
        block_masks.astype(jnp.float32)[:, None, :, None], (nb, BLK, nb, BLK)
    ).reshape(tokens, tokens)
    rows = lax.broadcasted_iota(jnp.int32, (tokens, tokens), 0)
    cols = lax.broadcasted_iota(jnp.int32, (tokens, tokens), 1)
    return jnp.where(cols <= rows, gate, 0.0)


def on_device(clean, delta, cotangent, w_query, w_key, w_value, masks):
    f32, bf16 = jnp.float32, jnp.bfloat16
    tok = clean.shape[0]
    feat = w_query.shape[1]
    half = feat // 2
    heads = half // DH
    rows_dev = w_query.shape[0]
    k = lax.axis_index("core")
    c = lax.axis_index("chip")
    chips = lax.axis_size("chip")
    first = k == 0

    x_in = (clean.astype(f32) + delta.astype(f32)).astype(bf16)
    x_pair = jnp.concatenate([x_in, swap(x_in)], axis=0)

    def cols(w, which):
        return lax.dynamic_slice_in_dim(w, which * half, half, axis=1)

    def chip_block(mats):
        mine = jnp.concatenate([cols(w, k) for w in mats], axis=1)
        recv = swap(jnp.concatenate([cols(w, 1 - k) for w in mats], axis=1))
        block = jnp.zeros((2 * rows_dev, mine.shape[1]), mine.dtype)
        block = lax.dynamic_update_slice_in_dim(block, mine, k * rows_dev, axis=0)
        return lax.dynamic_update_slice_in_dim(block, recv, (1 - k) * rows_dev, axis=0)

    span = 2 * rows_dev
    block = chip_block((w_query, w_key, w_value))
    parity = lax.axis_index("groups") % 2
    w_half = jnp.zeros((chips * span, block.shape[1]), bf16)
    for src, offset, piece in ring_gather(block, chips, c, parity):
        w_half = lax.dynamic_update_slice_in_dim(w_half, piece, src * span + offset, axis=0)
    projected = jnp.dot(x_pair, w_half, preferred_element_type=f32).astype(bf16)
    projected = projected.reshape(2, tok, 3, heads, DH)
    query = projected[:, :, 0]
    key = projected[:, :, 1]
    value = projected[:, :, 2]

    local = jnp.einsum("jthd,jthe->jhde", key, value, preferred_element_type=f32)
    state0 = exclusive_scan(local[0] + local[1], chips, False)
    state_mine = jnp.where(first, state0, state0 + local[1])
    state_other = jnp.where(first, state0 + local[0], state0)
    state_b = jnp.stack([state_mine, state_other]).astype(bf16)

    pair_masks = jnp.stack([masks[0], swap(masks[0])])
    allow = jax.vmap(dense_allow, in_axes=(0, None))(pair_masks, tok)

    scores = jnp.einsum("jthd,jshd->jhts", query, key, preferred_element_type=f32)
    attn = (scores * allow[:, None]).astype(bf16)
    mixed = jnp.einsum("jhts,jshd->jthd", attn, value, preferred_element_type=f32)
    mixed = mixed + jnp.einsum("jthd,jhde->jthe", query, state_b, preferred_element_type=f32)
    root = jnp.sqrt(jnp.mean(mixed * mixed, axis=-1, keepdims=True) + EPSILON)
    normed = mixed / root

    out_b = normed.astype(bf16).reshape(2, tok, half)
    out_recv = swap(out_b[1])
    output = jnp.where(
        first,
        jnp.concatenate([out_b[0], out_recv], axis=1),
        jnp.concatenate([out_recv, out_b[0]], axis=1),
    )

    cot = cotangent.reshape(tok, 2, half)
    cot_mine = jnp.where(first, cot[:, 0], cot[:, 1])
    cot_other = jnp.where(first, cot[:, 1], cot[:, 0])
    grad_out = jnp.stack([cot_mine, swap(cot_other)]).astype(f32).reshape(2, tok, heads, DH)
    d_mixed = (grad_out - normed * jnp.mean(grad_out * normed, axis=-1, keepdims=True)) / root
    d_mixed_b = d_mixed.astype(bf16)
    grad_local = jnp.einsum("jthd,jthe->jhde", query, d_mixed_b, preferred_element_type=f32)

    later1 = exclusive_scan(grad_local[0] + grad_local[1], chips, True)
    later_mine = jnp.where(first, later1 + grad_local[1], later1)
    later_other = jnp.where(first, later1, later1 + grad_local[0])
    later_b = jnp.stack([later_mine, later_other]).astype(bf16)

    d_attn = (
        jnp.einsum("jthe,jshe->jhts", d_mixed_b, value, preferred_element_type=f32) * allow[:, None]
    ).astype(bf16)
    d_query = jnp.einsum("jhts,jshd->jthd", d_attn, key, preferred_element_type=f32)
    d_query = d_query + jnp.einsum("jthe,jhde->jthd", d_mixed_b, state_b, preferred_element_type=f32)
    d_key = jnp.einsum("jhts,jthd->jshd", d_attn, query, preferred_element_type=f32)
    d_key = d_key + jnp.einsum("jshe,jhde->jshd", value, later_b, preferred_element_type=f32)
    d_value = jnp.einsum("jhts,jthe->jshe", attn, d_mixed_b, preferred_element_type=f32)
    d_value = d_value + jnp.einsum("jshd,jhde->jshe", key, later_b, preferred_element_type=f32)
    d_proj = jnp.stack([d_query, d_key, d_value], axis=2).astype(bf16).reshape(2, tok, 3 * half)

    def grad_rows(j):
        return lax.dot_general(d_proj[j], w_half, (((1,), (1,)), ((), ())), preferred_element_type=f32)

    received = swap(grad_rows(1))
    grad_input = (grad_rows(0) + received).astype(bf16)
    return (output, grad_input)


def solution(mesh):
    groups = mesh.shape["groups"]
    seq = mesh.shape["seq"]
    devices = np.asarray(mesh.devices).reshape(groups, seq // 2, 2)
    inner = Mesh(devices, TOKENS)
    rows = P(TOKENS, None)
    weights = P(("chip", "core"), None)
    return jax.shard_map(
        on_device,
        mesh=inner,
        in_specs=(rows, rows, rows, weights, weights, weights, P(TOKENS, None, None)),
        out_specs=(rows, rows),
        check_vma=False,
    )
```

```python
import jax
import jax.numpy as jnp
import numpy as np
from jax import lax
from jax.sharding import Mesh
from jax.sharding import PartitionSpec as P

DH = 128
BLK = 128

EPSILON = 1e-06

TOKENS = ("groups", "chip", "core")


def swap(x):
    return lax.ppermute(x, "core", [(0, 1), (1, 0)])


def ring_order(chips):
    if chips % 2:
        return list(range(chips))
    return list(range(0, chips, 2)) + list(range(chips - 1, 0, -2))


def ring_gather(block, chips, c, p):
    order = ring_order(chips)
    place = np.zeros(chips, np.int32)
    place[np.asarray(order)] = np.arange(chips)
    order_t = jnp.asarray(order, jnp.int32)
    here = jnp.asarray(place)[c]
    ahead = [(order[p_], order[(p_ + 1) % chips]) for p_ in range(chips)]
    behind = [(order[p_], order[(p_ - 1) % chips]) for p_ in range(chips)]
    share = block.shape[1] // 3
    width = block.shape[1] - share
    groups = lax.axis_size("groups")
    partner = [(g, g ^ 1) for g in range(groups)]

    def land(piece):
        sent = lax.dynamic_slice_in_dim(piece, p * share, share, axis=1)
        return (piece, lax.ppermute(sent, "groups", partner))

    fwd = lax.dynamic_slice_in_dim(block, p * share, width, axis=1)
    got = [(c, (fwd, lax.dynamic_slice_in_dim(block, (1 - p) * width, share, axis=1)))]
    bwd = fwd
    for step in range(1, chips // 2 + 1):
        fwd = lax.ppermute(fwd, "chip", ahead)
        got.append((order_t[(here - step) % chips], land(fwd)))
        if step <= (chips - 1) // 2:
            bwd = lax.ppermute(bwd, "chip", behind)
            got.append((order_t[(here + step) % chips], land(bwd)))
    return got


def exclusive_scan(total, chips, reverse):
    flat = total.reshape(chips, -1)
    got = lax.all_to_all(flat, "chip", 0, 0)
    if reverse:
        got = got[::-1]
    run = jnp.cumsum(got[:-1], axis=0)
    before = jnp.concatenate([jnp.zeros_like(got[:1]), run], axis=0)
    if reverse:
        before = before[::-1]
    back = lax.all_to_all(before, "chip", 0, 0)
    return back.reshape(total.shape)


def dense_allow(block_masks, tokens):
    nb = tokens // BLK
    gate = jnp.broadcast_to(
        block_masks.astype(jnp.float32)[:, None, :, None], (nb, BLK, nb, BLK)
    ).reshape(tokens, tokens)
    rows = lax.broadcasted_iota(jnp.int32, (tokens, tokens), 0)
    cols = lax.broadcasted_iota(jnp.int32, (tokens, tokens), 1)
    return jnp.where(cols <= rows, gate, 0.0)


def on_device(clean, delta, cotangent, w_query, w_key, w_value, masks):
    f32, bf16 = jnp.float32, jnp.bfloat16
    tok = clean.shape[0]
    feat = w_query.shape[1]
    half = feat // 2
    heads = half // DH
    rows_dev = w_query.shape[0]
    k = lax.axis_index("core")
    c = lax.axis_index("chip")
    chips = lax.axis_size("chip")
    first = k == 0

    x_in = (clean.astype(f32) + delta.astype(f32)).astype(bf16)
    x_pair = jnp.concatenate([x_in, swap(x_in)], axis=0)

    def cols(w, which):
        return lax.dynamic_slice_in_dim(w, which * half, half, axis=1)

    def chip_block(mats):
        mine = jnp.concatenate([cols(w, k) for w in mats], axis=1)
        recv = swap(jnp.concatenate([cols(w, 1 - k) for w in mats], axis=1))
        block = jnp.zeros((2 * rows_dev, mine.shape[1]), mine.dtype)
        block = lax.dynamic_update_slice_in_dim(block, mine, k * rows_dev, axis=0)
        return lax.dynamic_update_slice_in_dim(block, recv, (1 - k) * rows_dev, axis=0)

    span = 2 * rows_dev
    block = chip_block((w_query, w_key, w_value))
    parity = lax.axis_index("groups") % 2
    share = half
    width = 2 * half
    w_ring = jnp.zeros((chips * span, width), bf16)
    w_x = jnp.zeros((chips * span, share), bf16)
    for src, (ringed, swapped) in ring_gather(block, chips, c, parity):
        w_ring = lax.dynamic_update_slice_in_dim(w_ring, ringed, src * span, axis=0)
        w_x = lax.dynamic_update_slice_in_dim(w_x, swapped, src * span, axis=0)
    p_ring = jnp.dot(x_pair, w_ring, preferred_element_type=f32).astype(bf16)
    p_x = jnp.dot(x_pair, w_x, preferred_element_type=f32).astype(bf16)
    projected = jnp.where(
        parity == 0,
        jnp.concatenate([p_ring, p_x], axis=1),
        jnp.concatenate([p_x, p_ring], axis=1),
    )
    projected = projected.reshape(2, tok, 3, heads, DH)
    query = projected[:, :, 0]
    key = projected[:, :, 1]
    value = projected[:, :, 2]

    local = jnp.einsum("jthd,jthe->jhde", key, value, preferred_element_type=f32)
    state0 = exclusive_scan(local[0] + local[1], chips, False)
    state_mine = jnp.where(first, state0, state0 + local[1])
    state_other = jnp.where(first, state0 + local[0], state0)
    state_b = jnp.stack([state_mine, state_other]).astype(bf16)

    pair_masks = jnp.stack([masks[0], swap(masks[0])])
    allow = jax.vmap(dense_allow, in_axes=(0, None))(pair_masks, tok)

    scores = jnp.einsum("jthd,jshd->jhts", query, key, preferred_element_type=f32)
    attn = (scores * allow[:, None]).astype(bf16)
    mixed = jnp.einsum("jhts,jshd->jthd", attn, value, preferred_element_type=f32)
    mixed = mixed + jnp.einsum("jthd,jhde->jthe", query, state_b, preferred_element_type=f32)
    root = jnp.sqrt(jnp.mean(mixed * mixed, axis=-1, keepdims=True) + EPSILON)
    normed = mixed / root

    out_b = normed.astype(bf16).reshape(2, tok, half)
    out_recv = swap(out_b[1])
    output = jnp.where(
        first,
        jnp.concatenate([out_b[0], out_recv], axis=1),
        jnp.concatenate([out_recv, out_b[0]], axis=1),
    )

    cot = cotangent.reshape(tok, 2, half)
    cot_mine = jnp.where(first, cot[:, 0], cot[:, 1])
    cot_other = jnp.where(first, cot[:, 1], cot[:, 0])
    grad_out = jnp.stack([cot_mine, swap(cot_other)]).astype(f32).reshape(2, tok, heads, DH)
    d_mixed = (grad_out - normed * jnp.mean(grad_out * normed, axis=-1, keepdims=True)) / root
    d_mixed_b = d_mixed.astype(bf16)
    grad_local = jnp.einsum("jthd,jthe->jhde", query, d_mixed_b, preferred_element_type=f32)

    later1 = exclusive_scan(grad_local[0] + grad_local[1], chips, True)
    later_mine = jnp.where(first, later1 + grad_local[1], later1)
    later_other = jnp.where(first, later1, later1 + grad_local[0])
    later_b = jnp.stack([later_mine, later_other]).astype(bf16)

    d_attn = (
        jnp.einsum("jthe,jshe->jhts", d_mixed_b, value, preferred_element_type=f32) * allow[:, None]
    ).astype(bf16)
    d_query = jnp.einsum("jhts,jshd->jthd", d_attn, key, preferred_element_type=f32)
    d_query = d_query + jnp.einsum("jthe,jhde->jthd", d_mixed_b, state_b, preferred_element_type=f32)
    d_key = jnp.einsum("jhts,jthd->jshd", d_attn, query, preferred_element_type=f32)
    d_key = d_key + jnp.einsum("jshe,jhde->jshd", value, later_b, preferred_element_type=f32)
    d_value = jnp.einsum("jhts,jthe->jshe", attn, d_mixed_b, preferred_element_type=f32)
    d_value = d_value + jnp.einsum("jshd,jhde->jshe", key, later_b, preferred_element_type=f32)
    d_proj = jnp.stack([d_query, d_key, d_value], axis=2).astype(bf16).reshape(2, tok, 3 * half)

    def grad_rows(j):
        d_ring = lax.dynamic_slice_in_dim(d_proj[j], parity * share, width, axis=1)
        d_x = lax.dynamic_slice_in_dim(d_proj[j], (1 - parity) * width, share, axis=1)
        g = lax.dot_general(d_ring, w_ring, (((1,), (1,)), ((), ())), preferred_element_type=f32)
        return g + lax.dot_general(d_x, w_x, (((1,), (1,)), ((), ())), preferred_element_type=f32)

    received = swap(grad_rows(1))
    grad_input = (grad_rows(0) + received).astype(bf16)
    return (output, grad_input)


def solution(mesh):
    groups = mesh.shape["groups"]
    seq = mesh.shape["seq"]
    devices = np.asarray(mesh.devices).reshape(groups, seq // 2, 2)
    inner = Mesh(devices, TOKENS)
    rows = P(TOKENS, None)
    weights = P(("chip", "core"), None)
    return jax.shard_map(
        on_device,
        mesh=inner,
        in_specs=(rows, rows, rows, weights, weights, weights, P(TOKENS, None, None)),
        out_specs=(rows, rows),
        check_vma=False,
    )
```

```python
import jax
import jax.numpy as jnp
import numpy as np
from jax import lax
from jax.sharding import Mesh
from jax.sharding import PartitionSpec as P

DH = 128
BLK = 128

EPSILON = 1e-06

TOKENS = ("groups", "chip", "core")


def swap(x):
    return lax.ppermute(x, "core", [(0, 1), (1, 0)])


def ring_order(chips):
    if chips % 2:
        return list(range(chips))
    return list(range(0, chips, 2)) + list(range(chips - 1, 0, -2))


def ring_gather(block, chips, c, p):
    order = ring_order(chips)
    place = np.zeros(chips, np.int32)
    place[np.asarray(order)] = np.arange(chips)
    order_t = jnp.asarray(order, jnp.int32)
    here = jnp.asarray(place)[c]
    ahead = [(order[p_], order[(p_ + 1) % chips]) for p_ in range(chips)]
    behind = [(order[p_], order[(p_ - 1) % chips]) for p_ in range(chips)]
    share = block.shape[1] // 3
    width = block.shape[1] - share
    groups = lax.axis_size("groups")
    partner = [(g, g ^ 1) for g in range(groups)]

    def land(piece):
        sent = lax.dynamic_slice_in_dim(piece, p * share, share, axis=1)
        return (piece, lax.ppermute(sent, "groups", partner))

    fwd = lax.dynamic_slice_in_dim(block, p * share, width, axis=1)
    got = [(c, (fwd, lax.dynamic_slice_in_dim(block, (1 - p) * width, share, axis=1)))]
    bwd = fwd
    for step in range(1, chips // 2 + 1):
        fwd = lax.ppermute(fwd, "chip", ahead)
        got.append((order_t[(here - step) % chips], land(fwd)))
        if step <= (chips - 1) // 2:
            bwd = lax.ppermute(bwd, "chip", behind)
            got.append((order_t[(here + step) % chips], land(bwd)))
    return got


def exclusive_scan(total, chips, reverse):
    incl = total
    excl = jnp.zeros_like(total)
    d = 1
    while d < chips:
        if reverse:
            perm = [(i, i - d) for i in range(d, chips)]
        else:
            perm = [(i, i + d) for i in range(chips - d)]
        got = lax.ppermute(incl, "chip", perm)
        incl = incl + got
        excl = excl + got
        d *= 2
    return excl


def dense_allow(block_masks, tokens):
    nb = tokens // BLK
    gate = jnp.broadcast_to(
        block_masks.astype(jnp.float32)[:, None, :, None], (nb, BLK, nb, BLK)
    ).reshape(tokens, tokens)
    rows = lax.broadcasted_iota(jnp.int32, (tokens, tokens), 0)
    cols = lax.broadcasted_iota(jnp.int32, (tokens, tokens), 1)
    return jnp.where(cols <= rows, gate, 0.0)


def on_device(clean, delta, cotangent, w_query, w_key, w_value, masks):
    f32, bf16 = jnp.float32, jnp.bfloat16
    tok = clean.shape[0]
    feat = w_query.shape[1]
    half = feat // 2
    heads = half // DH
    rows_dev = w_query.shape[0]
    k = lax.axis_index("core")
    c = lax.axis_index("chip")
    chips = lax.axis_size("chip")
    first = k == 0

    x_in = (clean.astype(f32) + delta.astype(f32)).astype(bf16)
    x_pair = jnp.concatenate([x_in, swap(x_in)], axis=0)

    def cols(w, which):
        return lax.dynamic_slice_in_dim(w, which * half, half, axis=1)

    def chip_block(mats):
        mine = jnp.concatenate([cols(w, k) for w in mats], axis=1)
        recv = swap(jnp.concatenate([cols(w, 1 - k) for w in mats], axis=1))
        block = jnp.zeros((2 * rows_dev, mine.shape[1]), mine.dtype)
        block = lax.dynamic_update_slice_in_dim(block, mine, k * rows_dev, axis=0)
        return lax.dynamic_update_slice_in_dim(block, recv, (1 - k) * rows_dev, axis=0)

    span = 2 * rows_dev
    block = chip_block((w_query, w_key, w_value))
    parity = lax.axis_index("groups") % 2
    share = half
    width = 2 * half
    w_ring = jnp.zeros((chips * span, width), bf16)
    w_x = jnp.zeros((chips * span, share), bf16)
    p_ring = None
    p_x = None
    for src, (ringed, swapped) in ring_gather(block, chips, c, parity):
        w_ring = lax.dynamic_update_slice_in_dim(w_ring, ringed, src * span, axis=0)
        w_x = lax.dynamic_update_slice_in_dim(w_x, swapped, src * span, axis=0)
        x_cols = lax.dynamic_slice_in_dim(x_pair, src * span, span, axis=1)
        t_ring = jnp.dot(x_cols, ringed, preferred_element_type=f32)
        t_x = jnp.dot(x_cols, swapped, preferred_element_type=f32)
        p_ring = t_ring if p_ring is None else p_ring + t_ring
        p_x = t_x if p_x is None else p_x + t_x
    p_ring = p_ring.astype(bf16).reshape(2, tok, 2, heads, DH)
    p_x = p_x.astype(bf16).reshape(2, tok, heads, DH)
    query = jnp.where(parity == 0, p_ring[:, :, 0], p_x)
    key = jnp.where(parity == 0, p_ring[:, :, 1], p_ring[:, :, 0])
    value = jnp.where(parity == 0, p_x, p_ring[:, :, 1])

    local = jnp.einsum("jthd,jthe->jhde", key, value, preferred_element_type=f32)
    state0 = exclusive_scan(local[0] + local[1], chips, False)
    state_mine = jnp.where(first, state0, state0 + local[1])
    state_other = jnp.where(first, state0 + local[0], state0)
    state_b = jnp.stack([state_mine, state_other]).astype(bf16)

    pair_masks = jnp.stack([masks[0], swap(masks[0])])
    allow = jax.vmap(dense_allow, in_axes=(0, None))(pair_masks, tok)

    scores = jnp.einsum("jthd,jshd->jhts", query, key, preferred_element_type=f32)
    attn = (scores * allow[:, None]).astype(bf16)
    mixed = jnp.einsum("jhts,jshd->jthd", attn, value, preferred_element_type=f32)
    mixed = mixed + jnp.einsum("jthd,jhde->jthe", query, state_b, preferred_element_type=f32)
    root = jnp.sqrt(jnp.mean(mixed * mixed, axis=-1, keepdims=True) + EPSILON)
    normed = mixed / root

    out_b = normed.astype(bf16).reshape(2, tok, half)
    out_recv = swap(out_b[1])
    output = jnp.where(
        first,
        jnp.concatenate([out_b[0], out_recv], axis=1),
        jnp.concatenate([out_recv, out_b[0]], axis=1),
    )

    cot = cotangent.reshape(tok, 2, half)
    cot_mine = jnp.where(first, cot[:, 0], cot[:, 1])
    cot_other = jnp.where(first, cot[:, 1], cot[:, 0])
    grad_out = jnp.stack([cot_mine, swap(cot_other)]).astype(f32).reshape(2, tok, heads, DH)
    d_mixed = (grad_out - normed * jnp.mean(grad_out * normed, axis=-1, keepdims=True)) / root
    d_mixed_b = d_mixed.astype(bf16)
    grad_local = jnp.einsum("jthd,jthe->jhde", query, d_mixed_b, preferred_element_type=f32)

    later1 = exclusive_scan(grad_local[0] + grad_local[1], chips, True)
    later_mine = jnp.where(first, later1 + grad_local[1], later1)
    later_other = jnp.where(first, later1, later1 + grad_local[0])
    later_b = jnp.stack([later_mine, later_other]).astype(bf16)

    d_attn = (
        jnp.einsum("jthe,jshe->jhts", d_mixed_b, value, preferred_element_type=f32) * allow[:, None]
    ).astype(bf16)
    d_query = jnp.einsum("jhts,jshd->jthd", d_attn, key, preferred_element_type=f32)
    d_query = d_query + jnp.einsum("jthe,jhde->jthd", d_mixed_b, state_b, preferred_element_type=f32)
    d_key = jnp.einsum("jhts,jthd->jshd", d_attn, query, preferred_element_type=f32)
    d_key = d_key + jnp.einsum("jshe,jhde->jshd", value, later_b, preferred_element_type=f32)
    d_value = jnp.einsum("jhts,jthe->jshe", attn, d_mixed_b, preferred_element_type=f32)
    d_value = d_value + jnp.einsum("jshd,jhde->jshe", key, later_b, preferred_element_type=f32)
    d_proj = jnp.stack([d_query, d_key, d_value], axis=2).astype(bf16).reshape(2, tok, 3 * half)

    def grad_rows(j):
        d_ring = lax.dynamic_slice_in_dim(d_proj[j], parity * share, width, axis=1)
        d_x = lax.dynamic_slice_in_dim(d_proj[j], (1 - parity) * width, share, axis=1)
        g = lax.dot_general(d_ring, w_ring, (((1,), (1,)), ((), ())), preferred_element_type=f32)
        return g + lax.dot_general(d_x, w_x, (((1,), (1,)), ((), ())), preferred_element_type=f32)

    received = swap(grad_rows(1))
    grad_input = (grad_rows(0) + received).astype(bf16)
    return (output, grad_input)


def solution(mesh):
    groups = mesh.shape["groups"]
    seq = mesh.shape["seq"]
    devices = np.asarray(mesh.devices).reshape(groups, seq // 2, 2)
    inner = Mesh(devices, TOKENS)
    rows = P(TOKENS, None)
    weights = P(("chip", "core"), None)
    return jax.shard_map(
        on_device,
        mesh=inner,
        in_specs=(rows, rows, rows, weights, weights, weights, P(TOKENS, None, None)),
        out_specs=(rows, rows),
        check_vma=False,
    )
```

```python
import jax
import jax.numpy as jnp
import numpy as np
from jax import lax
from jax.sharding import Mesh
from jax.sharding import PartitionSpec as P

DH = 128
BLK = 128

EPSILON = 1e-06

TOKENS = ("groups", "chip", "core")


def swap(x):
    return lax.ppermute(x, "core", [(0, 1), (1, 0)])


def ring_order(chips):
    if chips % 2:
        return list(range(chips))
    return list(range(0, chips, 2)) + list(range(chips - 1, 0, -2))


def ring_gather(block, chips, c, p):
    order = ring_order(chips)
    place = np.zeros(chips, np.int32)
    place[np.asarray(order)] = np.arange(chips)
    order_t = jnp.asarray(order, jnp.int32)
    here = jnp.asarray(place)[c]
    ahead = [(order[p_], order[(p_ + 1) % chips]) for p_ in range(chips)]
    behind = [(order[p_], order[(p_ - 1) % chips]) for p_ in range(chips)]
    share = block.shape[1] // 3
    width = block.shape[1] - share
    groups = lax.axis_size("groups")
    partner = [(g, g ^ 1) for g in range(groups)]

    def land(piece):
        sent = lax.dynamic_slice_in_dim(piece, p * share, share, axis=1)
        return (piece, lax.ppermute(sent, "groups", partner))

    fwd = lax.dynamic_slice_in_dim(block, p * share, width, axis=1)
    got = [(c, (fwd, lax.dynamic_slice_in_dim(block, (1 - p) * width, share, axis=1)))]
    bwd = fwd
    for step in range(1, chips // 2 + 1):
        fwd = lax.ppermute(fwd, "chip", ahead)
        got.append((order_t[(here - step) % chips], land(fwd)))
        if step <= (chips - 1) // 2:
            bwd = lax.ppermute(bwd, "chip", behind)
            got.append((order_t[(here + step) % chips], land(bwd)))
    return got


def exclusive_scan(total, chips, reverse):
    incl = total
    excl = jnp.zeros_like(total)
    d = 1
    while d < chips:
        if reverse:
            perm = [(i, i - d) for i in range(d, chips)]
        else:
            perm = [(i, i + d) for i in range(chips - d)]
        got = lax.ppermute(incl, "chip", perm)
        incl = incl + got
        excl = excl + got
        d *= 2
    return excl


def dense_allow(block_masks, tokens):
    nb = tokens // BLK
    gate = jnp.broadcast_to(
        block_masks.astype(jnp.float32)[:, None, :, None], (nb, BLK, nb, BLK)
    ).reshape(tokens, tokens)
    rows = lax.broadcasted_iota(jnp.int32, (tokens, tokens), 0)
    cols = lax.broadcasted_iota(jnp.int32, (tokens, tokens), 1)
    return jnp.where(cols <= rows, gate, 0.0)


def on_device(clean, delta, cotangent, w_query, w_key, w_value, masks):
    f32, bf16 = jnp.float32, jnp.bfloat16
    tok = clean.shape[0]
    feat = w_query.shape[1]
    half = feat // 2
    heads = half // DH
    rows_dev = w_query.shape[0]
    k = lax.axis_index("core")
    c = lax.axis_index("chip")
    chips = lax.axis_size("chip")
    first = k == 0

    x_in = (clean.astype(f32) + delta.astype(f32)).astype(bf16)
    x_pair = jnp.concatenate([x_in, swap(x_in)], axis=0)

    def cols(w, which):
        return lax.dynamic_slice_in_dim(w, which * half, half, axis=1)

    def chip_block(mats):
        mine = jnp.concatenate([cols(w, k) for w in mats], axis=1)
        recv = swap(jnp.concatenate([cols(w, 1 - k) for w in mats], axis=1))
        block = jnp.zeros((2 * rows_dev, mine.shape[1]), mine.dtype)
        block = lax.dynamic_update_slice_in_dim(block, mine, k * rows_dev, axis=0)
        return lax.dynamic_update_slice_in_dim(block, recv, (1 - k) * rows_dev, axis=0)

    span = 2 * rows_dev
    block = chip_block((w_query, w_key, w_value))
    parity = lax.axis_index("groups") % 2
    share = half
    width = 2 * half
    w_ring = jnp.zeros((chips * span, width), bf16)
    w_x = jnp.zeros((chips * span, share), bf16)
    for src, (ringed, swapped) in ring_gather(block, chips, c, parity):
        w_ring = lax.dynamic_update_slice_in_dim(w_ring, ringed, src * span, axis=0)
        w_x = lax.dynamic_update_slice_in_dim(w_x, swapped, src * span, axis=0)
    p_ring = jnp.dot(x_pair, w_ring, preferred_element_type=f32).astype(bf16)
    p_x = jnp.dot(x_pair, w_x, preferred_element_type=f32).astype(bf16)
    projected = jnp.where(
        parity == 0,
        jnp.concatenate([p_ring, p_x], axis=1),
        jnp.concatenate([p_x, p_ring], axis=1),
    )
    projected = projected.reshape(2, tok, 3, heads, DH)
    query = projected[:, :, 0]
    key = projected[:, :, 1]
    value = projected[:, :, 2]

    local = jnp.einsum("jthd,jthe->jhde", key, value, preferred_element_type=f32)
    state0 = exclusive_scan(local[0] + local[1], chips, False)
    state_mine = jnp.where(first, state0, state0 + local[1])
    state_other = jnp.where(first, state0 + local[0], state0)
    state_b = jnp.stack([state_mine, state_other]).astype(bf16)

    pair_masks = jnp.stack([masks[0], swap(masks[0])])
    allow = jax.vmap(dense_allow, in_axes=(0, None))(pair_masks, tok)

    scores = jnp.einsum("jthd,jshd->jhts", query, key, preferred_element_type=f32)
    attn = (scores * allow[:, None]).astype(bf16)
    mixed = jnp.einsum("jhts,jshd->jthd", attn, value, preferred_element_type=f32)
    mixed = mixed + jnp.einsum("jthd,jhde->jthe", query, state_b, preferred_element_type=f32)
    root = jnp.sqrt(jnp.mean(mixed * mixed, axis=-1, keepdims=True) + EPSILON)
    normed = mixed / root

    out_b = normed.astype(bf16).reshape(2, tok, half)
    out_recv = swap(out_b[1])
    output = jnp.where(
        first,
        jnp.concatenate([out_b[0], out_recv], axis=1),
        jnp.concatenate([out_recv, out_b[0]], axis=1),
    )

    cot = cotangent.reshape(tok, 2, half)
    cot_mine = jnp.where(first, cot[:, 0], cot[:, 1])
    cot_other = jnp.where(first, cot[:, 1], cot[:, 0])
    grad_out = jnp.stack([cot_mine, swap(cot_other)]).astype(f32).reshape(2, tok, heads, DH)
    d_mixed = (grad_out - normed * jnp.mean(grad_out * normed, axis=-1, keepdims=True)) / root
    d_mixed_b = d_mixed.astype(bf16)
    grad_local = jnp.einsum("jthd,jthe->jhde", query, d_mixed_b, preferred_element_type=f32)

    later1 = exclusive_scan(grad_local[0] + grad_local[1], chips, True)
    later_mine = jnp.where(first, later1 + grad_local[1], later1)
    later_other = jnp.where(first, later1, later1 + grad_local[0])
    later_b = jnp.stack([later_mine, later_other]).astype(bf16)

    d_attn = (
        jnp.einsum("jthe,jshe->jhts", d_mixed_b, value, preferred_element_type=f32) * allow[:, None]
    ).astype(bf16)
    d_query = jnp.einsum("jhts,jshd->jthd", d_attn, key, preferred_element_type=f32)
    d_query = d_query + jnp.einsum("jthe,jhde->jthd", d_mixed_b, state_b, preferred_element_type=f32)
    d_key = jnp.einsum("jhts,jthd->jshd", d_attn, query, preferred_element_type=f32)
    d_key = d_key + jnp.einsum("jshe,jhde->jshd", value, later_b, preferred_element_type=f32)
    d_value = jnp.einsum("jhts,jthe->jshe", attn, d_mixed_b, preferred_element_type=f32)
    d_value = d_value + jnp.einsum("jshd,jhde->jshe", key, later_b, preferred_element_type=f32)
    d_proj = jnp.stack([d_query, d_key, d_value], axis=2).astype(bf16).reshape(2, tok, 3 * half)

    def grad_rows(j):
        d_ring = lax.dynamic_slice_in_dim(d_proj[j], parity * share, width, axis=1)
        d_x = lax.dynamic_slice_in_dim(d_proj[j], (1 - parity) * width, share, axis=1)
        g = lax.dot_general(d_ring, w_ring, (((1,), (1,)), ((), ())), preferred_element_type=f32)
        return g + lax.dot_general(d_x, w_x, (((1,), (1,)), ((), ())), preferred_element_type=f32)

    received = swap(grad_rows(1))
    own, received = lax.optimization_barrier((grad_rows(0), received))
    grad_input = (own + received).astype(bf16)
    return (output, grad_input)


def solution(mesh):
    groups = mesh.shape["groups"]
    seq = mesh.shape["seq"]
    devices = np.asarray(mesh.devices).reshape(groups, seq // 2, 2)
    inner = Mesh(devices, TOKENS)
    rows = P(TOKENS, None)
    weights = P(("chip", "core"), None)
    return jax.shard_map(
        on_device,
        mesh=inner,
        in_specs=(rows, rows, rows, weights, weights, weights, P(TOKENS, None, None)),
        out_specs=(rows, rows),
        check_vma=False,
    )
```

```python
import jax
import jax.numpy as jnp
import numpy as np
from jax import lax
from jax.sharding import Mesh
from jax.sharding import PartitionSpec as P

DH = 128
BLK = 128

EPSILON = 1e-06

TOKENS = ("groups", "chip", "core")


def swap(x):
    return lax.ppermute(x, "core", [(0, 1), (1, 0)])


def ring_order(chips):
    if chips % 2:
        return list(range(chips))
    return list(range(0, chips, 2)) + list(range(chips - 1, 0, -2))


def ring_gather(block, chips, c, p):
    order = ring_order(chips)
    place = np.zeros(chips, np.int32)
    place[np.asarray(order)] = np.arange(chips)
    order_t = jnp.asarray(order, jnp.int32)
    here = jnp.asarray(place)[c]
    ahead = [(order[p_], order[(p_ + 1) % chips]) for p_ in range(chips)]
    behind = [(order[p_], order[(p_ - 1) % chips]) for p_ in range(chips)]
    share = block.shape[1] // 3
    width = block.shape[1] - share
    groups = lax.axis_size("groups")
    partner = [(g, g ^ 1) for g in range(groups)]

    def land(piece):
        sent = lax.dynamic_slice_in_dim(piece, p * share, share, axis=1)
        return (piece, lax.ppermute(sent, "groups", partner))

    fwd = lax.dynamic_slice_in_dim(block, p * share, width, axis=1)
    got = [(c, (fwd, lax.dynamic_slice_in_dim(block, (1 - p) * width, share, axis=1)))]
    bwd = fwd
    for step in range(1, chips // 2 + 1):
        fwd = lax.ppermute(fwd, "chip", ahead)
        got.append((order_t[(here - step) % chips], land(fwd)))
        if step <= (chips - 1) // 2:
            bwd = lax.ppermute(bwd, "chip", behind)
            got.append((order_t[(here + step) % chips], land(bwd)))
    return got


def exclusive_scan(total, chips, reverse):
    incl = total
    excl = jnp.zeros_like(total)
    d = 1
    while d < chips:
        if reverse:
            perm = [(i, i - d) for i in range(d, chips)]
        else:
            perm = [(i, i + d) for i in range(chips - d)]
        got = lax.ppermute(incl, "chip", perm)
        incl = incl + got
        excl = excl + got
        d *= 2
    return excl


def dense_allow(block_masks, tokens):
    nb = tokens // BLK
    gate = jnp.broadcast_to(
        block_masks.astype(jnp.float32)[:, None, :, None], (nb, BLK, nb, BLK)
    ).reshape(tokens, tokens)
    rows = lax.broadcasted_iota(jnp.int32, (tokens, tokens), 0)
    cols = lax.broadcasted_iota(jnp.int32, (tokens, tokens), 1)
    return jnp.where(cols <= rows, gate, 0.0)


def on_device(clean, delta, cotangent, w_query, w_key, w_value, masks):
    f32, bf16 = jnp.float32, jnp.bfloat16
    tok = clean.shape[0]
    feat = w_query.shape[1]
    half = feat // 2
    heads = half // DH
    rows_dev = w_query.shape[0]
    k = lax.axis_index("core")
    c = lax.axis_index("chip")
    chips = lax.axis_size("chip")
    first = k == 0

    x_in = (clean.astype(f32) + delta.astype(f32)).astype(bf16)
    x_pair = jnp.concatenate([x_in, swap(x_in)], axis=0)

    def cols(w, which):
        return lax.dynamic_slice_in_dim(w, which * half, half, axis=1)

    def chip_block(mats):
        mine = jnp.concatenate([cols(w, k) for w in mats], axis=1)
        recv = swap(jnp.concatenate([cols(w, 1 - k) for w in mats], axis=1))
        block = jnp.zeros((2 * rows_dev, mine.shape[1]), mine.dtype)
        block = lax.dynamic_update_slice_in_dim(block, mine, k * rows_dev, axis=0)
        return lax.dynamic_update_slice_in_dim(block, recv, (1 - k) * rows_dev, axis=0)

    span = 2 * rows_dev
    block = chip_block((w_query, w_key, w_value))
    parity = lax.axis_index("groups") % 2
    share = half
    width = 2 * half
    w_ring = jnp.zeros((chips * span, width), bf16)
    w_x = jnp.zeros((chips * span, share), bf16)
    for src, (ringed, swapped) in ring_gather(block, chips, c, parity):
        w_ring = lax.dynamic_update_slice_in_dim(w_ring, ringed, src * span, axis=0)
        w_x = lax.dynamic_update_slice_in_dim(w_x, swapped, src * span, axis=0)
    p_ring = jnp.dot(x_pair, w_ring, preferred_element_type=f32).astype(bf16)
    p_x = jnp.dot(x_pair, w_x, preferred_element_type=f32).astype(bf16)
    projected = jnp.where(
        parity == 0,
        jnp.concatenate([p_ring, p_x], axis=1),
        jnp.concatenate([p_x, p_ring], axis=1),
    )
    projected = projected.reshape(2, tok, 3, heads, DH)
    query = projected[:, :, 0]
    key = projected[:, :, 1]
    value = projected[:, :, 2]

    local = jnp.einsum("jthd,jthe->jhde", key, value, preferred_element_type=f32)
    state0 = exclusive_scan(local[0] + local[1], chips, False)
    state_mine = jnp.where(first, state0, state0 + local[1])
    state_other = jnp.where(first, state0 + local[0], state0)
    state_b = jnp.stack([state_mine, state_other]).astype(bf16)

    pair_masks = jnp.stack([masks[0], swap(masks[0])])
    allow = jax.vmap(dense_allow, in_axes=(0, None))(pair_masks, tok)

    scores = jnp.einsum("jthd,jshd->jhts", query, key, preferred_element_type=f32)
    attn = (scores * allow[:, None]).astype(bf16)
    mixed = jnp.einsum("jhts,jshd->jthd", attn, value, preferred_element_type=f32)
    mixed = mixed + jnp.einsum("jthd,jhde->jthe", query, state_b, preferred_element_type=f32)
    root = jnp.sqrt(jnp.mean(mixed * mixed, axis=-1, keepdims=True) + EPSILON)
    normed = mixed / root

    out_b = normed.astype(bf16).reshape(2, tok, half)
    out_recv = swap(out_b[1])
    output = jnp.where(
        first,
        jnp.concatenate([out_b[0], out_recv], axis=1),
        jnp.concatenate([out_recv, out_b[0]], axis=1),
    )

    cot = cotangent.reshape(tok, 2, half)
    cot_mine = jnp.where(first, cot[:, 0], cot[:, 1])
    cot_other = jnp.where(first, cot[:, 1], cot[:, 0])
    grad_out = jnp.stack([cot_mine, swap(cot_other)]).astype(f32).reshape(2, tok, heads, DH)
    d_mixed = (grad_out - normed * jnp.mean(grad_out * normed, axis=-1, keepdims=True)) / root
    d_mixed_b = d_mixed.astype(bf16)
    grad_local = jnp.einsum("jthd,jthe->jhde", query, d_mixed_b, preferred_element_type=f32)
    output, grad_local = lax.optimization_barrier((output, grad_local))

    later1 = exclusive_scan(grad_local[0] + grad_local[1], chips, True)
    later_mine = jnp.where(first, later1 + grad_local[1], later1)
    later_other = jnp.where(first, later1, later1 + grad_local[0])
    later_b = jnp.stack([later_mine, later_other]).astype(bf16)

    d_attn = (
        jnp.einsum("jthe,jshe->jhts", d_mixed_b, value, preferred_element_type=f32) * allow[:, None]
    ).astype(bf16)
    d_query = jnp.einsum("jhts,jshd->jthd", d_attn, key, preferred_element_type=f32)
    d_query = d_query + jnp.einsum("jthe,jhde->jthd", d_mixed_b, state_b, preferred_element_type=f32)
    d_key = jnp.einsum("jhts,jthd->jshd", d_attn, query, preferred_element_type=f32)
    d_key = d_key + jnp.einsum("jshe,jhde->jshd", value, later_b, preferred_element_type=f32)
    d_value = jnp.einsum("jhts,jthe->jshe", attn, d_mixed_b, preferred_element_type=f32)
    d_value = d_value + jnp.einsum("jshd,jhde->jshe", key, later_b, preferred_element_type=f32)
    d_proj = jnp.stack([d_query, d_key, d_value], axis=2).astype(bf16).reshape(2, tok, 3 * half)

    def grad_rows(j):
        d_ring = lax.dynamic_slice_in_dim(d_proj[j], parity * share, width, axis=1)
        d_x = lax.dynamic_slice_in_dim(d_proj[j], (1 - parity) * width, share, axis=1)
        g = lax.dot_general(d_ring, w_ring, (((1,), (1,)), ((), ())), preferred_element_type=f32)
        return g + lax.dot_general(d_x, w_x, (((1,), (1,)), ((), ())), preferred_element_type=f32)

    received = swap(grad_rows(1))
    own, received = lax.optimization_barrier((grad_rows(0), received))
    grad_input = (own + received).astype(bf16)
    return (output, grad_input)


def solution(mesh):
    groups = mesh.shape["groups"]
    seq = mesh.shape["seq"]
    devices = np.asarray(mesh.devices).reshape(groups, seq // 2, 2)
    inner = Mesh(devices, TOKENS)
    rows = P(TOKENS, None)
    weights = P(("chip", "core"), None)
    return jax.shard_map(
        on_device,
        mesh=inner,
        in_specs=(rows, rows, rows, weights, weights, weights, P(TOKENS, None, None)),
        out_specs=(rows, rows),
        check_vma=False,
    )
```

```python
import jax
import jax.numpy as jnp
import numpy as np
from jax import lax
from jax.sharding import Mesh
from jax.sharding import PartitionSpec as P

DH = 128
BLK = 128

EPSILON = 1e-06

TOKENS = ("groups", "chip", "core")


def swap(x):
    return lax.ppermute(x, "core", [(0, 1), (1, 0)])


def ring_order(chips):
    if chips % 2:
        return list(range(chips))
    return list(range(0, chips, 2)) + list(range(chips - 1, 0, -2))


def ring_gather(block, chips, c, p):
    order = ring_order(chips)
    place = np.zeros(chips, np.int32)
    place[np.asarray(order)] = np.arange(chips)
    order_t = jnp.asarray(order, jnp.int32)
    here = jnp.asarray(place)[c]
    ahead = [(order[p_], order[(p_ + 1) % chips]) for p_ in range(chips)]
    behind = [(order[p_], order[(p_ - 1) % chips]) for p_ in range(chips)]
    share = block.shape[1] // 3
    width = block.shape[1] - share
    groups = lax.axis_size("groups")
    partner = [(g, g ^ 1) for g in range(groups)]

    def land(piece):
        sent = lax.dynamic_slice_in_dim(piece, p * share, share, axis=1)
        return (piece, lax.ppermute(sent, "groups", partner))

    fwd = lax.dynamic_slice_in_dim(block, p * share, width, axis=1)
    got = [(c, (fwd, lax.dynamic_slice_in_dim(block, (1 - p) * width, share, axis=1)))]
    bwd = fwd
    for step in range(1, chips // 2 + 1):
        fwd = lax.ppermute(fwd, "chip", ahead)
        got.append((order_t[(here - step) % chips], land(fwd)))
        if step <= (chips - 1) // 2:
            bwd = lax.ppermute(bwd, "chip", behind)
            got.append((order_t[(here + step) % chips], land(bwd)))
    return got


def exclusive_scan(total, chips, reverse):
    incl = total
    excl = jnp.zeros_like(total)
    d = 1
    while d < chips:
        if reverse:
            perm = [(i, i - d) for i in range(d, chips)]
        else:
            perm = [(i, i + d) for i in range(chips - d)]
        got = lax.ppermute(incl, "chip", perm)
        incl = incl + got
        excl = excl + got
        d *= 2
    return excl


def dense_allow(block_masks, tokens):
    nb = tokens // BLK
    gate = jnp.broadcast_to(
        block_masks.astype(jnp.float32)[:, None, :, None], (nb, BLK, nb, BLK)
    ).reshape(tokens, tokens)
    rows = lax.broadcasted_iota(jnp.int32, (tokens, tokens), 0)
    cols = lax.broadcasted_iota(jnp.int32, (tokens, tokens), 1)
    return jnp.where(cols <= rows, gate, 0.0)


def on_device(clean, delta, cotangent, w_query, w_key, w_value, masks):
    f32, bf16 = jnp.float32, jnp.bfloat16
    tok = clean.shape[0]
    feat = w_query.shape[1]
    half = feat // 2
    heads = half // DH
    rows_dev = w_query.shape[0]
    k = lax.axis_index("core")
    c = lax.axis_index("chip")
    chips = lax.axis_size("chip")
    first = k == 0

    x_in = (clean.astype(f32) + delta.astype(f32)).astype(bf16)
    x_pair = jnp.concatenate([x_in, swap(x_in)], axis=0)

    def cols(w, which):
        return lax.dynamic_slice_in_dim(w, which * half, half, axis=1)

    def chip_block(mats):
        mine = jnp.concatenate([cols(w, k) for w in mats], axis=1)
        recv = swap(jnp.concatenate([cols(w, 1 - k) for w in mats], axis=1))
        block = jnp.zeros((2 * rows_dev, mine.shape[1]), mine.dtype)
        block = lax.dynamic_update_slice_in_dim(block, mine, k * rows_dev, axis=0)
        return lax.dynamic_update_slice_in_dim(block, recv, (1 - k) * rows_dev, axis=0)

    span = 2 * rows_dev
    block = chip_block((w_query, w_key, w_value))
    parity = lax.axis_index("groups") % 2
    share = half
    width = 2 * half
    mats = [jnp.zeros((chips * span, share), bf16) for _ in range(3)]
    for src, (ringed, swapped) in ring_gather(block, chips, c, parity):
        lower, upper = ringed[:, :share], ringed[:, share:]
        parts = (
            jnp.where(parity == 0, lower, swapped),
            jnp.where(parity == 0, upper, lower),
            jnp.where(parity == 0, swapped, upper),
        )
        mats = [lax.dynamic_update_slice_in_dim(m, part, src * span, axis=0) for m, part in zip(mats, parts)]
    w_q, w_k, w_v = mats

    def project(w):
        return jnp.dot(x_pair, w, preferred_element_type=f32).astype(bf16).reshape(2, tok, heads, DH)

    key = project(w_k)
    value = project(w_v)
    query = project(w_q)

    local = jnp.einsum("jthd,jthe->jhde", key, value, preferred_element_type=f32)
    state0 = exclusive_scan(local[0] + local[1], chips, False)
    state_mine = jnp.where(first, state0, state0 + local[1])
    state_other = jnp.where(first, state0 + local[0], state0)
    state_b = jnp.stack([state_mine, state_other]).astype(bf16)

    pair_masks = jnp.stack([masks[0], swap(masks[0])])
    allow = jax.vmap(dense_allow, in_axes=(0, None))(pair_masks, tok)

    scores = jnp.einsum("jthd,jshd->jhts", query, key, preferred_element_type=f32)
    attn = (scores * allow[:, None]).astype(bf16)
    mixed = jnp.einsum("jhts,jshd->jthd", attn, value, preferred_element_type=f32)
    mixed = mixed + jnp.einsum("jthd,jhde->jthe", query, state_b, preferred_element_type=f32)
    root = jnp.sqrt(jnp.mean(mixed * mixed, axis=-1, keepdims=True) + EPSILON)
    normed = mixed / root

    out_b = normed.astype(bf16).reshape(2, tok, half)
    out_recv = swap(out_b[1])
    output = jnp.where(
        first,
        jnp.concatenate([out_b[0], out_recv], axis=1),
        jnp.concatenate([out_recv, out_b[0]], axis=1),
    )

    cot = cotangent.reshape(tok, 2, half)
    cot_mine = jnp.where(first, cot[:, 0], cot[:, 1])
    cot_other = jnp.where(first, cot[:, 1], cot[:, 0])
    grad_out = jnp.stack([cot_mine, swap(cot_other)]).astype(f32).reshape(2, tok, heads, DH)
    d_mixed = (grad_out - normed * jnp.mean(grad_out * normed, axis=-1, keepdims=True)) / root
    d_mixed_b = d_mixed.astype(bf16)
    grad_local = jnp.einsum("jthd,jthe->jhde", query, d_mixed_b, preferred_element_type=f32)
    output, grad_local = lax.optimization_barrier((output, grad_local))

    later1 = exclusive_scan(grad_local[0] + grad_local[1], chips, True)
    later_mine = jnp.where(first, later1 + grad_local[1], later1)
    later_other = jnp.where(first, later1, later1 + grad_local[0])
    later_b = jnp.stack([later_mine, later_other]).astype(bf16)

    d_attn = (
        jnp.einsum("jthe,jshe->jhts", d_mixed_b, value, preferred_element_type=f32) * allow[:, None]
    ).astype(bf16)
    d_query = jnp.einsum("jhts,jshd->jthd", d_attn, key, preferred_element_type=f32)
    d_query = d_query + jnp.einsum("jthe,jhde->jthd", d_mixed_b, state_b, preferred_element_type=f32)
    d_key = jnp.einsum("jhts,jthd->jshd", d_attn, query, preferred_element_type=f32)
    d_key = d_key + jnp.einsum("jshe,jhde->jshd", value, later_b, preferred_element_type=f32)
    d_value = jnp.einsum("jhts,jthe->jshe", attn, d_mixed_b, preferred_element_type=f32)
    d_value = d_value + jnp.einsum("jshd,jhde->jshe", key, later_b, preferred_element_type=f32)
    dq_b = d_query.astype(bf16).reshape(2, tok, half)
    dk_b = d_key.astype(bf16).reshape(2, tok, half)
    dv_b = d_value.astype(bf16).reshape(2, tok, half)

    def grad_rows(j):
        dims = (((1,), (1,)), ((), ()))
        g = lax.dot_general(dq_b[j], w_q, dims, preferred_element_type=f32)
        g = g + lax.dot_general(dk_b[j], w_k, dims, preferred_element_type=f32)
        return g + lax.dot_general(dv_b[j], w_v, dims, preferred_element_type=f32)

    received = swap(grad_rows(1))
    own, received = lax.optimization_barrier((grad_rows(0), received))
    grad_input = (own + received).astype(bf16)
    return (output, grad_input)


def solution(mesh):
    groups = mesh.shape["groups"]
    seq = mesh.shape["seq"]
    devices = np.asarray(mesh.devices).reshape(groups, seq // 2, 2)
    inner = Mesh(devices, TOKENS)
    rows = P(TOKENS, None)
    weights = P(("chip", "core"), None)
    return jax.shard_map(
        on_device,
        mesh=inner,
        in_specs=(rows, rows, rows, weights, weights, weights, P(TOKENS, None, None)),
        out_specs=(rows, rows),
        check_vma=False,
    )
```

```python
import jax
import jax.numpy as jnp
import numpy as np
from jax import lax
from jax.sharding import Mesh
from jax.sharding import PartitionSpec as P

DH = 128
BLK = 128

EPSILON = 1e-06

TOKENS = ("groups", "chip", "core")


def swap(x):
    return lax.ppermute(x, "core", [(0, 1), (1, 0)])


def ring_order(chips):
    if chips % 2:
        return list(range(chips))
    return list(range(0, chips, 2)) + list(range(chips - 1, 0, -2))


def ring_gather(block, chips, c, p):
    order = ring_order(chips)
    place = np.zeros(chips, np.int32)
    place[np.asarray(order)] = np.arange(chips)
    order_t = jnp.asarray(order, jnp.int32)
    here = jnp.asarray(place)[c]
    ahead = [(order[p_], order[(p_ + 1) % chips]) for p_ in range(chips)]
    behind = [(order[p_], order[(p_ - 1) % chips]) for p_ in range(chips)]
    share = block.shape[1] // 3
    width = block.shape[1] - share
    groups = lax.axis_size("groups")
    partner = [(g, g ^ 1) for g in range(groups)]

    def land(piece):
        sent = lax.dynamic_slice_in_dim(piece, p * share, share, axis=1)
        return (piece, lax.ppermute(sent, "groups", partner))

    fwd = lax.dynamic_slice_in_dim(block, p * share, width, axis=1)
    got = [(c, (fwd, lax.dynamic_slice_in_dim(block, (1 - p) * width, share, axis=1)))]
    bwd = fwd
    for step in range(1, chips // 2 + 1):
        fwd = lax.ppermute(fwd, "chip", ahead)
        got.append((order_t[(here - step) % chips], land(fwd)))
        if step <= (chips - 1) // 2:
            bwd = lax.ppermute(bwd, "chip", behind)
            got.append((order_t[(here + step) % chips], land(bwd)))
    return got


def exclusive_scan(total, chips, reverse):
    incl = total
    excl = jnp.zeros_like(total)
    d = 1
    while d < chips:
        if reverse:
            perm = [(i, i - d) for i in range(d, chips)]
        else:
            perm = [(i, i + d) for i in range(chips - d)]
        got = lax.ppermute(incl, "chip", perm)
        incl = incl + got
        excl = excl + got
        d *= 2
    return excl


def dense_allow(block_masks, tokens):
    nb = tokens // BLK
    gate = jnp.broadcast_to(
        block_masks.astype(jnp.float32)[:, None, :, None], (nb, BLK, nb, BLK)
    ).reshape(tokens, tokens)
    rows = lax.broadcasted_iota(jnp.int32, (tokens, tokens), 0)
    cols = lax.broadcasted_iota(jnp.int32, (tokens, tokens), 1)
    return jnp.where(cols <= rows, gate, 0.0)


def on_device(clean, delta, cotangent, w_query, w_key, w_value, masks):
    f32, bf16 = jnp.float32, jnp.bfloat16
    tok = clean.shape[0]
    feat = w_query.shape[1]
    half = feat // 2
    heads = half // DH
    rows_dev = w_query.shape[0]
    k = lax.axis_index("core")
    c = lax.axis_index("chip")
    chips = lax.axis_size("chip")
    first = k == 0

    x_in = (clean.astype(f32) + delta.astype(f32)).astype(bf16)
    x_pair = jnp.concatenate([x_in, swap(x_in)], axis=0)

    def cols(w, which):
        return lax.dynamic_slice_in_dim(w, which * half, half, axis=1)

    def chip_block(mats):
        mine = jnp.concatenate([cols(w, k) for w in mats], axis=1)
        recv = swap(jnp.concatenate([cols(w, 1 - k) for w in mats], axis=1))
        block = jnp.zeros((2 * rows_dev, mine.shape[1]), mine.dtype)
        block = lax.dynamic_update_slice_in_dim(block, mine, k * rows_dev, axis=0)
        return lax.dynamic_update_slice_in_dim(block, recv, (1 - k) * rows_dev, axis=0)

    span = 2 * rows_dev
    block = chip_block((w_query, w_key, w_value))
    parity = lax.axis_index("groups") % 2
    share = half
    width = 2 * half
    mats = [jnp.zeros((chips * span, share), bf16) for _ in range(3)]
    for src, (ringed, swapped) in ring_gather(block, chips, c, parity):
        lower, upper = ringed[:, :share], ringed[:, share:]
        parts = (
            jnp.where(parity == 0, lower, swapped),
            jnp.where(parity == 0, upper, lower),
            jnp.where(parity == 0, swapped, upper),
        )
        mats = [lax.dynamic_update_slice_in_dim(m, part, src * span, axis=0) for m, part in zip(mats, parts)]
    w_q, w_k, w_v = mats

    def project(w):
        return jnp.dot(x_pair, w, preferred_element_type=f32).astype(bf16).reshape(2, tok, heads, DH)

    key = project(w_k)
    value = project(w_v)
    query = project(w_q)

    local = jnp.einsum("jthd,jthe->jhde", key, value, preferred_element_type=f32)
    state0 = exclusive_scan(local[0] + local[1], chips, False)
    state_mine = jnp.where(first, state0, state0 + local[1])
    state_other = jnp.where(first, state0 + local[0], state0)
    state_b = jnp.stack([state_mine, state_other]).astype(bf16)

    pair_masks = jnp.stack([masks[0], swap(masks[0])])
    allow = jax.vmap(dense_allow, in_axes=(0, None))(pair_masks, tok)

    scores = jnp.einsum("jthd,jshd->jhts", query, key, preferred_element_type=f32)
    attn = (scores * allow[:, None]).astype(bf16)
    mixed = jnp.einsum("jhts,jshd->jthd", attn, value, preferred_element_type=f32)
    mixed = mixed + jnp.einsum("jthd,jhde->jthe", query, state_b, preferred_element_type=f32)
    root = jnp.sqrt(jnp.mean(mixed * mixed, axis=-1, keepdims=True) + EPSILON)
    normed = mixed / root

    out_b = normed.astype(bf16).reshape(2, tok, half)
    cot = cotangent.reshape(tok, 2, half)
    cot_mine = jnp.where(first, cot[:, 0], cot[:, 1])
    cot_other = jnp.where(first, cot[:, 1], cot[:, 0])
    grad_out = jnp.stack([cot_mine, swap(cot_other)]).astype(f32).reshape(2, tok, heads, DH)
    d_mixed = (grad_out - normed * jnp.mean(grad_out * normed, axis=-1, keepdims=True)) / root
    d_mixed_b = d_mixed.astype(bf16)
    grad_local = jnp.einsum("jthd,jthe->jhde", query, d_mixed_b, preferred_element_type=f32)

    later1 = exclusive_scan(grad_local[0] + grad_local[1], chips, True)
    later_mine = jnp.where(first, later1 + grad_local[1], later1)
    later_other = jnp.where(first, later1, later1 + grad_local[0])
    later_b = jnp.stack([later_mine, later_other]).astype(bf16)
    out_send, later_b = lax.optimization_barrier((out_b[1], later_b))
    out_recv = swap(out_send)
    output = jnp.where(
        first,
        jnp.concatenate([out_b[0], out_recv], axis=1),
        jnp.concatenate([out_recv, out_b[0]], axis=1),
    )

    d_attn = (
        jnp.einsum("jthe,jshe->jhts", d_mixed_b, value, preferred_element_type=f32) * allow[:, None]
    ).astype(bf16)
    d_query = jnp.einsum("jhts,jshd->jthd", d_attn, key, preferred_element_type=f32)
    d_query = d_query + jnp.einsum("jthe,jhde->jthd", d_mixed_b, state_b, preferred_element_type=f32)
    d_key = jnp.einsum("jhts,jthd->jshd", d_attn, query, preferred_element_type=f32)
    d_key = d_key + jnp.einsum("jshe,jhde->jshd", value, later_b, preferred_element_type=f32)
    d_value = jnp.einsum("jhts,jthe->jshe", attn, d_mixed_b, preferred_element_type=f32)
    d_value = d_value + jnp.einsum("jshd,jhde->jshe", key, later_b, preferred_element_type=f32)
    dq_b = d_query.astype(bf16).reshape(2, tok, half)
    dk_b = d_key.astype(bf16).reshape(2, tok, half)
    dv_b = d_value.astype(bf16).reshape(2, tok, half)

    def grad_rows(j):
        dims = (((1,), (1,)), ((), ()))
        g = lax.dot_general(dq_b[j], w_q, dims, preferred_element_type=f32)
        g = g + lax.dot_general(dk_b[j], w_k, dims, preferred_element_type=f32)
        return g + lax.dot_general(dv_b[j], w_v, dims, preferred_element_type=f32)

    received = swap(grad_rows(1))
    own, received = lax.optimization_barrier((grad_rows(0), received))
    grad_input = (own + received).astype(bf16)
    return (output, grad_input)


def solution(mesh):
    groups = mesh.shape["groups"]
    seq = mesh.shape["seq"]
    devices = np.asarray(mesh.devices).reshape(groups, seq // 2, 2)
    inner = Mesh(devices, TOKENS)
    rows = P(TOKENS, None)
    weights = P(("chip", "core"), None)
    return jax.shard_map(
        on_device,
        mesh=inner,
        in_specs=(rows, rows, rows, weights, weights, weights, P(TOKENS, None, None)),
        out_specs=(rows, rows),
        check_vma=False,
    )
```

```python
import jax
import jax.numpy as jnp
import numpy as np
from jax import lax
from jax.sharding import Mesh
from jax.sharding import PartitionSpec as P

DH = 128
BLK = 128

EPSILON = 1e-06

TOKENS = ("groups", "chip", "core")


def swap(x):
    return lax.ppermute(x, "core", [(0, 1), (1, 0)])


def ring_order(chips):
    if chips % 2:
        return list(range(chips))
    return list(range(0, chips, 2)) + list(range(chips - 1, 0, -2))


def ring_gather(block, chips, c, p):
    order = ring_order(chips)
    place = np.zeros(chips, np.int32)
    place[np.asarray(order)] = np.arange(chips)
    order_t = jnp.asarray(order, jnp.int32)
    here = jnp.asarray(place)[c]
    ahead = [(order[p_], order[(p_ + 1) % chips]) for p_ in range(chips)]
    behind = [(order[p_], order[(p_ - 1) % chips]) for p_ in range(chips)]
    share = block.shape[1] // 3
    width = block.shape[1] - share
    groups = lax.axis_size("groups")
    partner = [(g, g ^ 1) for g in range(groups)]

    def land(piece):
        sent = lax.dynamic_slice_in_dim(piece, p * share, share, axis=1)
        return (piece, lax.ppermute(sent, "groups", partner))

    fwd = lax.dynamic_slice_in_dim(block, p * share, width, axis=1)
    got = [(c, (fwd, lax.dynamic_slice_in_dim(block, (1 - p) * width, share, axis=1)))]
    bwd = fwd
    for step in range(1, chips // 2 + 1):
        fwd = lax.ppermute(fwd, "chip", ahead)
        got.append((order_t[(here - step) % chips], land(fwd)))
        if step <= (chips - 1) // 2:
            bwd = lax.ppermute(bwd, "chip", behind)
            got.append((order_t[(here + step) % chips], land(bwd)))
    return got


def exclusive_scan(total, chips, reverse):
    incl = total
    excl = jnp.zeros_like(total)
    d = 1
    while d < chips:
        if reverse:
            perm = [(i, i - d) for i in range(d, chips)]
        else:
            perm = [(i, i + d) for i in range(chips - d)]
        got = lax.ppermute(incl, "chip", perm)
        incl = incl + got
        excl = excl + got
        d *= 2
    return excl


def dense_allow(block_masks, tokens):
    nb = tokens // BLK
    gate = jnp.broadcast_to(
        block_masks.astype(jnp.float32)[:, None, :, None], (nb, BLK, nb, BLK)
    ).reshape(tokens, tokens)
    rows = lax.broadcasted_iota(jnp.int32, (tokens, tokens), 0)
    cols = lax.broadcasted_iota(jnp.int32, (tokens, tokens), 1)
    return jnp.where(cols <= rows, gate, 0.0)


def on_device(clean, delta, cotangent, w_query, w_key, w_value, masks):
    f32, bf16 = jnp.float32, jnp.bfloat16
    tok = clean.shape[0]
    feat = w_query.shape[1]
    half = feat // 2
    heads = half // DH
    rows_dev = w_query.shape[0]
    k = lax.axis_index("core")
    c = lax.axis_index("chip")
    chips = lax.axis_size("chip")
    first = k == 0

    x_in = (clean.astype(f32) + delta.astype(f32)).astype(bf16)
    x_pair = jnp.concatenate([x_in, swap(x_in)], axis=0)

    def cols(w, which):
        return lax.dynamic_slice_in_dim(w, which * half, half, axis=1)

    def chip_block(mats):
        mine = jnp.concatenate([cols(w, k) for w in mats], axis=1)
        recv = swap(jnp.concatenate([cols(w, 1 - k) for w in mats], axis=1))
        block = jnp.zeros((2 * rows_dev, mine.shape[1]), mine.dtype)
        block = lax.dynamic_update_slice_in_dim(block, mine, k * rows_dev, axis=0)
        return lax.dynamic_update_slice_in_dim(block, recv, (1 - k) * rows_dev, axis=0)

    span = 2 * rows_dev
    block = chip_block((w_query, w_key, w_value))
    parity = lax.axis_index("groups") % 2
    share = half
    width = 2 * half
    w_ring = jnp.zeros((chips * span, width), bf16)
    w_x = jnp.zeros((chips * span, share), bf16)
    for src, (ringed, swapped) in ring_gather(block, chips, c, parity):
        w_ring = lax.dynamic_update_slice_in_dim(w_ring, ringed, src * span, axis=0)
        w_x = lax.dynamic_update_slice_in_dim(w_x, swapped, src * span, axis=0)
    even = parity == 0

    def project(w):
        return jnp.dot(x_pair, w, preferred_element_type=f32).astype(bf16).reshape(2, tok, heads, DH)

    p_lo = project(w_ring[:, :share])
    p_hi = project(w_ring[:, share:])
    p_x = project(w_x)
    query = jnp.where(even, p_lo, p_x)
    key = jnp.where(even, p_hi, p_lo)
    value = jnp.where(even, p_x, p_hi)

    local = jnp.einsum("jthd,jthe->jhde", key, value, preferred_element_type=f32)
    state0 = exclusive_scan(local[0] + local[1], chips, False)
    state_mine = jnp.where(first, state0, state0 + local[1])
    state_other = jnp.where(first, state0 + local[0], state0)
    state_b = jnp.stack([state_mine, state_other]).astype(bf16)

    pair_masks = jnp.stack([masks[0], swap(masks[0])])
    allow = jax.vmap(dense_allow, in_axes=(0, None))(pair_masks, tok)

    scores = jnp.einsum("jthd,jshd->jhts", query, key, preferred_element_type=f32)
    attn = (scores * allow[:, None]).astype(bf16)
    mixed = jnp.einsum("jhts,jshd->jthd", attn, value, preferred_element_type=f32)
    mixed = mixed + jnp.einsum("jthd,jhde->jthe", query, state_b, preferred_element_type=f32)
    root = jnp.sqrt(jnp.mean(mixed * mixed, axis=-1, keepdims=True) + EPSILON)
    normed = mixed / root

    out_b = normed.astype(bf16).reshape(2, tok, half)
    cot = cotangent.reshape(tok, 2, half)
    cot_mine = jnp.where(first, cot[:, 0], cot[:, 1])
    cot_other = jnp.where(first, cot[:, 1], cot[:, 0])
    grad_out = jnp.stack([cot_mine, swap(cot_other)]).astype(f32).reshape(2, tok, heads, DH)
    d_mixed = (grad_out - normed * jnp.mean(grad_out * normed, axis=-1, keepdims=True)) / root
    d_mixed_b = d_mixed.astype(bf16)
    grad_local = jnp.einsum("jthd,jthe->jhde", query, d_mixed_b, preferred_element_type=f32)

    later1 = exclusive_scan(grad_local[0] + grad_local[1], chips, True)
    later_mine = jnp.where(first, later1 + grad_local[1], later1)
    later_other = jnp.where(first, later1, later1 + grad_local[0])
    later_b = jnp.stack([later_mine, later_other]).astype(bf16)
    out_send, later_b = lax.optimization_barrier((out_b[1], later_b))
    out_recv = swap(out_send)
    output = jnp.where(
        first,
        jnp.concatenate([out_b[0], out_recv], axis=1),
        jnp.concatenate([out_recv, out_b[0]], axis=1),
    )

    d_attn = (
        jnp.einsum("jthe,jshe->jhts", d_mixed_b, value, preferred_element_type=f32) * allow[:, None]
    ).astype(bf16)
    d_query = jnp.einsum("jhts,jshd->jthd", d_attn, key, preferred_element_type=f32)
    d_query = d_query + jnp.einsum("jthe,jhde->jthd", d_mixed_b, state_b, preferred_element_type=f32)
    d_key = jnp.einsum("jhts,jthd->jshd", d_attn, query, preferred_element_type=f32)
    d_key = d_key + jnp.einsum("jshe,jhde->jshd", value, later_b, preferred_element_type=f32)
    d_value = jnp.einsum("jhts,jthe->jshe", attn, d_mixed_b, preferred_element_type=f32)
    d_value = d_value + jnp.einsum("jshd,jhde->jshe", key, later_b, preferred_element_type=f32)
    dq_b = d_query.astype(bf16).reshape(2, tok, half)
    dk_b = d_key.astype(bf16).reshape(2, tok, half)
    dv_b = d_value.astype(bf16).reshape(2, tok, half)

    def grad_rows(j):
        dims = (((1,), (1,)), ((), ()))
        d_lo = jnp.where(even, dq_b[j], dk_b[j])
        d_hi = jnp.where(even, dk_b[j], dv_b[j])
        d_x = jnp.where(even, dv_b[j], dq_b[j])
        g = lax.dot_general(d_lo, w_ring[:, :share], dims, preferred_element_type=f32)
        g = g + lax.dot_general(d_hi, w_ring[:, share:], dims, preferred_element_type=f32)
        return g + lax.dot_general(d_x, w_x, dims, preferred_element_type=f32)

    received = swap(grad_rows(1))
    own, received = lax.optimization_barrier((grad_rows(0), received))
    grad_input = (own + received).astype(bf16)
    return (output, grad_input)


def solution(mesh):
    groups = mesh.shape["groups"]
    seq = mesh.shape["seq"]
    devices = np.asarray(mesh.devices).reshape(groups, seq // 2, 2)
    inner = Mesh(devices, TOKENS)
    rows = P(TOKENS, None)
    weights = P(("chip", "core"), None)
    return jax.shard_map(
        on_device,
        mesh=inner,
        in_specs=(rows, rows, rows, weights, weights, weights, P(TOKENS, None, None)),
        out_specs=(rows, rows),
        check_vma=False,
    )
```

```python
import jax
import jax.numpy as jnp
import numpy as np
from jax import lax
from jax.sharding import Mesh
from jax.sharding import PartitionSpec as P

DH = 128
BLK = 128

EPSILON = 1e-06

TOKENS = ("groups", "chip", "core")


def swap(x):
    return lax.ppermute(x, "core", [(0, 1), (1, 0)])


def ring_order(chips):
    if chips % 2:
        return list(range(chips))
    return list(range(0, chips, 2)) + list(range(chips - 1, 0, -2))


def ring_gather(block, chips, c, p):
    order = ring_order(chips)
    place = np.zeros(chips, np.int32)
    place[np.asarray(order)] = np.arange(chips)
    order_t = jnp.asarray(order, jnp.int32)
    here = jnp.asarray(place)[c]
    ahead = [(order[p_], order[(p_ + 1) % chips]) for p_ in range(chips)]
    behind = [(order[p_], order[(p_ - 1) % chips]) for p_ in range(chips)]
    share = block.shape[1] // 3
    width = block.shape[1] - share
    groups = lax.axis_size("groups")
    partner = [(g, g ^ 1) for g in range(groups)]

    def land(piece):
        sent = lax.dynamic_slice_in_dim(piece, p * share, share, axis=1)
        return (piece, lax.ppermute(sent, "groups", partner))

    fwd = lax.dynamic_slice_in_dim(block, p * share, width, axis=1)
    got = [(c, (fwd, lax.dynamic_slice_in_dim(block, (1 - p) * width, share, axis=1)))]
    bwd = fwd
    for step in range(1, chips // 2 + 1):
        fwd = lax.ppermute(fwd, "chip", ahead)
        got.append((order_t[(here - step) % chips], land(fwd)))
        if step <= (chips - 1) // 2:
            bwd = lax.ppermute(bwd, "chip", behind)
            got.append((order_t[(here + step) % chips], land(bwd)))
    return got


def exclusive_scan(total, chips, reverse):
    incl = total
    excl = jnp.zeros_like(total)
    d = 1
    while d < chips:
        if reverse:
            perm = [(i, i - d) for i in range(d, chips)]
        else:
            perm = [(i, i + d) for i in range(chips - d)]
        got = lax.ppermute(incl, "chip", perm)
        incl = incl + got
        excl = excl + got
        d *= 2
    return excl


def dense_allow(block_masks, tokens):
    nb = tokens // BLK
    gate = jnp.broadcast_to((block_masks != 0)[:, None, :, None], (nb, BLK, nb, BLK)).reshape(tokens, tokens)
    rows = lax.broadcasted_iota(jnp.int32, (tokens, tokens), 0)
    cols = lax.broadcasted_iota(jnp.int32, (tokens, tokens), 1)
    return gate & (cols <= rows)


def on_device(clean, delta, cotangent, w_query, w_key, w_value, masks):
    f32, bf16 = jnp.float32, jnp.bfloat16
    tok = clean.shape[0]
    feat = w_query.shape[1]
    half = feat // 2
    heads = half // DH
    rows_dev = w_query.shape[0]
    k = lax.axis_index("core")
    c = lax.axis_index("chip")
    chips = lax.axis_size("chip")
    first = k == 0

    x_in = (clean.astype(f32) + delta.astype(f32)).astype(bf16)
    x_pair = jnp.concatenate([x_in, swap(x_in)], axis=0)

    def cols(w, which):
        return lax.dynamic_slice_in_dim(w, which * half, half, axis=1)

    def chip_block(mats):
        mine = jnp.concatenate([cols(w, k) for w in mats], axis=1)
        recv = swap(jnp.concatenate([cols(w, 1 - k) for w in mats], axis=1))
        block = jnp.zeros((2 * rows_dev, mine.shape[1]), mine.dtype)
        block = lax.dynamic_update_slice_in_dim(block, mine, k * rows_dev, axis=0)
        return lax.dynamic_update_slice_in_dim(block, recv, (1 - k) * rows_dev, axis=0)

    span = 2 * rows_dev
    block = chip_block((w_query, w_key, w_value))
    parity = lax.axis_index("groups") % 2
    share = half
    width = 2 * half
    w_ring = jnp.zeros((chips * span, width), bf16)
    w_x = jnp.zeros((chips * span, share), bf16)
    for src, (ringed, swapped) in ring_gather(block, chips, c, parity):
        w_ring = lax.dynamic_update_slice_in_dim(w_ring, ringed, src * span, axis=0)
        w_x = lax.dynamic_update_slice_in_dim(w_x, swapped, src * span, axis=0)
    even = parity == 0

    def project(w):
        return jnp.dot(x_pair, w, preferred_element_type=f32).astype(bf16).reshape(2, tok, heads, DH)

    p_lo = project(w_ring[:, :share])
    p_hi = project(w_ring[:, share:])
    p_x = project(w_x)
    query = jnp.where(even, p_lo, p_x)
    key = jnp.where(even, p_hi, p_lo)
    value = jnp.where(even, p_x, p_hi)

    local = jnp.einsum("jthd,jthe->jhde", key, value, preferred_element_type=f32)
    state0 = exclusive_scan(local[0] + local[1], chips, False)
    state_mine = jnp.where(first, state0, state0 + local[1])
    state_other = jnp.where(first, state0 + local[0], state0)
    state_b = jnp.stack([state_mine, state_other]).astype(bf16)

    pair_masks = jnp.stack([masks[0], swap(masks[0])])
    allow = jax.vmap(dense_allow, in_axes=(0, None))(pair_masks, tok)

    scores = jnp.einsum("jthd,jshd->jhts", query, key, preferred_element_type=f32)
    attn = jnp.where(allow[:, None], scores, 0.0).astype(bf16)
    mixed = jnp.einsum("jhts,jshd->jthd", attn, value, preferred_element_type=f32)
    mixed = mixed + jnp.einsum("jthd,jhde->jthe", query, state_b, preferred_element_type=f32)
    root = jnp.sqrt(jnp.mean(mixed * mixed, axis=-1, keepdims=True) + EPSILON)
    normed = mixed / root

    out_b = normed.astype(bf16).reshape(2, tok, half)
    cot = cotangent.reshape(tok, 2, half)
    cot_mine = jnp.where(first, cot[:, 0], cot[:, 1])
    cot_other = jnp.where(first, cot[:, 1], cot[:, 0])
    grad_out = jnp.stack([cot_mine, swap(cot_other)]).astype(f32).reshape(2, tok, heads, DH)
    d_mixed = (grad_out - normed * jnp.mean(grad_out * normed, axis=-1, keepdims=True)) / root
    d_mixed_b = d_mixed.astype(bf16)
    grad_local = jnp.einsum("jthd,jthe->jhde", query, d_mixed_b, preferred_element_type=f32)

    later1 = exclusive_scan(grad_local[0] + grad_local[1], chips, True)
    later_mine = jnp.where(first, later1 + grad_local[1], later1)
    later_other = jnp.where(first, later1, later1 + grad_local[0])
    later_b = jnp.stack([later_mine, later_other]).astype(bf16)
    out_send, later_b = lax.optimization_barrier((out_b[1], later_b))
    out_recv = swap(out_send)
    output = jnp.where(
        first,
        jnp.concatenate([out_b[0], out_recv], axis=1),
        jnp.concatenate([out_recv, out_b[0]], axis=1),
    )

    d_scores = jnp.einsum("jthe,jshe->jhts", d_mixed_b, value, preferred_element_type=f32)
    d_attn = jnp.where(allow[:, None], d_scores, 0.0).astype(bf16)
    d_query = jnp.einsum("jhts,jshd->jthd", d_attn, key, preferred_element_type=f32)
    d_query = d_query + jnp.einsum("jthe,jhde->jthd", d_mixed_b, state_b, preferred_element_type=f32)
    d_key = jnp.einsum("jhts,jthd->jshd", d_attn, query, preferred_element_type=f32)
    d_key = d_key + jnp.einsum("jshe,jhde->jshd", value, later_b, preferred_element_type=f32)
    d_value = jnp.einsum("jhts,jthe->jshe", attn, d_mixed_b, preferred_element_type=f32)
    d_value = d_value + jnp.einsum("jshd,jhde->jshe", key, later_b, preferred_element_type=f32)
    dq_b = d_query.astype(bf16).reshape(2, tok, half)
    dk_b = d_key.astype(bf16).reshape(2, tok, half)
    dv_b = d_value.astype(bf16).reshape(2, tok, half)

    def grad_rows(j):
        dims = (((1,), (1,)), ((), ()))
        d_lo = jnp.where(even, dq_b[j], dk_b[j])
        d_hi = jnp.where(even, dk_b[j], dv_b[j])
        d_x = jnp.where(even, dv_b[j], dq_b[j])
        g = lax.dot_general(d_lo, w_ring[:, :share], dims, preferred_element_type=f32)
        g = g + lax.dot_general(d_hi, w_ring[:, share:], dims, preferred_element_type=f32)
        return g + lax.dot_general(d_x, w_x, dims, preferred_element_type=f32)

    received = swap(grad_rows(1))
    own, received = lax.optimization_barrier((grad_rows(0), received))
    grad_input = (own + received).astype(bf16)
    return (output, grad_input)


def solution(mesh):
    groups = mesh.shape["groups"]
    seq = mesh.shape["seq"]
    devices = np.asarray(mesh.devices).reshape(groups, seq // 2, 2)
    inner = Mesh(devices, TOKENS)
    rows = P(TOKENS, None)
    weights = P(("chip", "core"), None)
    return jax.shard_map(
        on_device,
        mesh=inner,
        in_specs=(rows, rows, rows, weights, weights, weights, P(TOKENS, None, None)),
        out_specs=(rows, rows),
        check_vma=False,
    )
```

```python
import jax
import jax.numpy as jnp
import numpy as np
from jax import lax
from jax.sharding import Mesh
from jax.sharding import PartitionSpec as P

DH = 128
BLK = 128

EPSILON = 1e-06

TOKENS = ("groups", "chip", "core")


def swap(x):
    return lax.ppermute(x, "core", [(0, 1), (1, 0)])


def ring_order(chips):
    if chips % 2:
        return list(range(chips))
    return list(range(0, chips, 2)) + list(range(chips - 1, 0, -2))


def ring_gather(block, chips, c, p):
    order = ring_order(chips)
    place = np.zeros(chips, np.int32)
    place[np.asarray(order)] = np.arange(chips)
    order_t = jnp.asarray(order, jnp.int32)
    here = jnp.asarray(place)[c]
    ahead = [(order[p_], order[(p_ + 1) % chips]) for p_ in range(chips)]
    behind = [(order[p_], order[(p_ - 1) % chips]) for p_ in range(chips)]
    share = block.shape[1] // 3
    width = block.shape[1] - share
    groups = lax.axis_size("groups")
    partner = [(g, g ^ 1) for g in range(groups)]

    def land(piece):
        sent = lax.dynamic_slice_in_dim(piece, p * share, share, axis=1)
        return (piece, lax.ppermute(sent, "groups", partner))

    fwd = lax.dynamic_slice_in_dim(block, p * share, width, axis=1)
    got = [(c, (fwd, lax.dynamic_slice_in_dim(block, (1 - p) * width, share, axis=1)))]
    bwd = fwd
    for step in range(1, chips // 2 + 1):
        fwd = lax.ppermute(fwd, "chip", ahead)
        got.append((order_t[(here - step) % chips], land(fwd)))
        if step <= (chips - 1) // 2:
            bwd = lax.ppermute(bwd, "chip", behind)
            got.append((order_t[(here + step) % chips], land(bwd)))
    return got


def exclusive_scan(total, chips, reverse):
    incl = total
    excl = jnp.zeros_like(total)
    d = 1
    while d < chips:
        if reverse:
            perm = [(i, i - d) for i in range(d, chips)]
        else:
            perm = [(i, i + d) for i in range(chips - d)]
        got = lax.ppermute(incl, "chip", perm)
        incl = incl + got
        excl = excl + got
        d *= 2
    return excl


def dense_allow(block_masks, tokens):
    nb = tokens // BLK
    gate = jnp.broadcast_to((block_masks != 0)[:, None, :, None], (nb, BLK, nb, BLK)).reshape(tokens, tokens)
    rows = lax.broadcasted_iota(jnp.int32, (tokens, tokens), 0)
    cols = lax.broadcasted_iota(jnp.int32, (tokens, tokens), 1)
    return gate & (cols <= rows)


def on_device(clean, delta, cotangent, w_query, w_key, w_value, masks):
    f32, bf16 = jnp.float32, jnp.bfloat16
    tok = clean.shape[0]
    feat = w_query.shape[1]
    half = feat // 2
    heads = half // DH
    rows_dev = w_query.shape[0]
    k = lax.axis_index("core")
    c = lax.axis_index("chip")
    chips = lax.axis_size("chip")
    first = k == 0

    x_in = (clean.astype(f32) + delta.astype(f32)).astype(bf16)
    x_pair = jnp.concatenate([x_in, swap(x_in)], axis=0)

    def cols(w, which):
        return lax.dynamic_slice_in_dim(w, which * half, half, axis=1)

    def chip_block(mats):
        mine = jnp.concatenate([cols(w, k) for w in mats], axis=1)
        recv = swap(jnp.concatenate([cols(w, 1 - k) for w in mats], axis=1))
        block = jnp.zeros((2 * rows_dev, mine.shape[1]), mine.dtype)
        block = lax.dynamic_update_slice_in_dim(block, mine, k * rows_dev, axis=0)
        return lax.dynamic_update_slice_in_dim(block, recv, (1 - k) * rows_dev, axis=0)

    span = 2 * rows_dev
    block = chip_block((w_query, w_key, w_value))
    parity = lax.axis_index("groups") % 2
    share = half
    width = 2 * half
    w_all = jnp.zeros((chips * span, width + share), bf16)
    for src, (ringed, swapped) in ring_gather(block, chips, c, parity):
        w_all = lax.dynamic_update_slice(w_all, ringed, (src * span, 0))
        w_all = lax.dynamic_update_slice(w_all, swapped, (src * span, width))
    at_q = parity * width
    at_k = (1 - parity) * share
    at_v = width - parity * share
    p_all = jnp.dot(x_pair, w_all, preferred_element_type=f32).astype(bf16)

    def pick(at):
        return lax.dynamic_slice_in_dim(p_all, at, share, axis=1).reshape(2, tok, heads, DH)

    query = pick(at_q)
    key = pick(at_k)
    value = pick(at_v)

    local = jnp.einsum("jthd,jthe->jhde", key, value, preferred_element_type=f32)
    state0 = exclusive_scan(local[0] + local[1], chips, False)
    state_mine = jnp.where(first, state0, state0 + local[1])
    state_other = jnp.where(first, state0 + local[0], state0)
    state_b = jnp.stack([state_mine, state_other]).astype(bf16)

    pair_masks = jnp.stack([masks[0], swap(masks[0])])
    allow = jax.vmap(dense_allow, in_axes=(0, None))(pair_masks, tok)

    scores = jnp.einsum("jthd,jshd->jhts", query, key, preferred_element_type=f32)
    attn = jnp.where(allow[:, None], scores, 0.0).astype(bf16)
    mixed = jnp.einsum("jhts,jshd->jthd", attn, value, preferred_element_type=f32)
    mixed = mixed + jnp.einsum("jthd,jhde->jthe", query, state_b, preferred_element_type=f32)
    root = jnp.sqrt(jnp.mean(mixed * mixed, axis=-1, keepdims=True) + EPSILON)
    normed = mixed / root

    out_b = normed.astype(bf16).reshape(2, tok, half)
    cot = cotangent.reshape(tok, 2, half)
    cot_mine = jnp.where(first, cot[:, 0], cot[:, 1])
    cot_other = jnp.where(first, cot[:, 1], cot[:, 0])
    grad_out = jnp.stack([cot_mine, swap(cot_other)]).astype(f32).reshape(2, tok, heads, DH)
    d_mixed = (grad_out - normed * jnp.mean(grad_out * normed, axis=-1, keepdims=True)) / root
    d_mixed_b = d_mixed.astype(bf16)
    grad_local = jnp.einsum("jthd,jthe->jhde", query, d_mixed_b, preferred_element_type=f32)

    later1 = exclusive_scan(grad_local[0] + grad_local[1], chips, True)
    later_mine = jnp.where(first, later1 + grad_local[1], later1)
    later_other = jnp.where(first, later1, later1 + grad_local[0])
    later_b = jnp.stack([later_mine, later_other]).astype(bf16)
    out_send, later_b = lax.optimization_barrier((out_b[1], later_b))
    out_recv = swap(out_send)
    output = jnp.where(
        first,
        jnp.concatenate([out_b[0], out_recv], axis=1),
        jnp.concatenate([out_recv, out_b[0]], axis=1),
    )

    d_scores = jnp.einsum("jthe,jshe->jhts", d_mixed_b, value, preferred_element_type=f32)
    d_attn = jnp.where(allow[:, None], d_scores, 0.0).astype(bf16)
    d_query = jnp.einsum("jhts,jshd->jthd", d_attn, key, preferred_element_type=f32)
    d_query = d_query + jnp.einsum("jthe,jhde->jthd", d_mixed_b, state_b, preferred_element_type=f32)
    d_key = jnp.einsum("jhts,jthd->jshd", d_attn, query, preferred_element_type=f32)
    d_key = d_key + jnp.einsum("jshe,jhde->jshd", value, later_b, preferred_element_type=f32)
    d_value = jnp.einsum("jhts,jthe->jshe", attn, d_mixed_b, preferred_element_type=f32)
    d_value = d_value + jnp.einsum("jshd,jhde->jshe", key, later_b, preferred_element_type=f32)
    dq_b = d_query.astype(bf16).reshape(2, tok, half)
    dk_b = d_key.astype(bf16).reshape(2, tok, half)
    dv_b = d_value.astype(bf16).reshape(2, tok, half)

    def grad_rows(j):
        dims = (((1,), (1,)), ((), ()))
        g = None
        for d, at in ((dq_b[j], at_q), (dk_b[j], at_k), (dv_b[j], at_v)):
            w = lax.dynamic_slice_in_dim(w_all, at, share, axis=1)
            t = lax.dot_general(d, w, dims, preferred_element_type=f32)
            g = t if g is None else g + t
        return g

    received = swap(grad_rows(1))
    own, received = lax.optimization_barrier((grad_rows(0), received))
    grad_input = (own + received).astype(bf16)
    return (output, grad_input)


def solution(mesh):
    groups = mesh.shape["groups"]
    seq = mesh.shape["seq"]
    devices = np.asarray(mesh.devices).reshape(groups, seq // 2, 2)
    inner = Mesh(devices, TOKENS)
    rows = P(TOKENS, None)
    weights = P(("chip", "core"), None)
    return jax.shard_map(
        on_device,
        mesh=inner,
        in_specs=(rows, rows, rows, weights, weights, weights, P(TOKENS, None, None)),
        out_specs=(rows, rows),
        check_vma=False,
    )
```

```python
import jax
import jax.numpy as jnp
import numpy as np
from jax import lax
from jax.sharding import Mesh
from jax.sharding import PartitionSpec as P

DH = 128
BLK = 128

EPSILON = 1e-06

TOKENS = ("groups", "chip", "core")


def swap(x):
    return lax.ppermute(x, "core", [(0, 1), (1, 0)])


def ring_order(chips):
    if chips % 2:
        return list(range(chips))
    return list(range(0, chips, 2)) + list(range(chips - 1, 0, -2))


def ring_gather(block, chips, c, p):
    order = ring_order(chips)
    place = np.zeros(chips, np.int32)
    place[np.asarray(order)] = np.arange(chips)
    order_t = jnp.asarray(order, jnp.int32)
    here = jnp.asarray(place)[c]
    ahead = [(order[p_], order[(p_ + 1) % chips]) for p_ in range(chips)]
    behind = [(order[p_], order[(p_ - 1) % chips]) for p_ in range(chips)]
    share = block.shape[1] // 3
    width = block.shape[1] - share
    groups = lax.axis_size("groups")
    partner = [(g, g ^ 1) for g in range(groups)]

    def land(piece):
        sent = lax.dynamic_slice_in_dim(piece, p * share, share, axis=1)
        return (piece, lax.ppermute(sent, "groups", partner))

    fwd = lax.dynamic_slice_in_dim(block, p * share, width, axis=1)
    got = [(c, (fwd, lax.dynamic_slice_in_dim(block, (1 - p) * width, share, axis=1)))]
    bwd = fwd
    for step in range(1, chips // 2 + 1):
        fwd = lax.ppermute(fwd, "chip", ahead)
        got.append((order_t[(here - step) % chips], land(fwd)))
        if step <= (chips - 1) // 2:
            bwd = lax.ppermute(bwd, "chip", behind)
            got.append((order_t[(here + step) % chips], land(bwd)))
    return got


def exclusive_scan(total, chips, reverse, side=()):
    incl = total
    excl = jnp.zeros_like(total)
    d = 1
    while d < chips:
        if reverse:
            perm = [(i, i - d) for i in range(d, chips)]
        else:
            perm = [(i, i + d) for i in range(chips - d)]
        got = lax.ppermute(incl, "chip", perm)
        if d == 1:
            side, got = lax.optimization_barrier((side, got))
        incl = incl + got
        excl = excl + got
        d *= 2
    return excl, side


def dense_allow(block_masks, tokens):
    nb = tokens // BLK
    gate = jnp.broadcast_to((block_masks != 0)[:, None, :, None], (nb, BLK, nb, BLK)).reshape(tokens, tokens)
    rows = lax.broadcasted_iota(jnp.int32, (tokens, tokens), 0)
    cols = lax.broadcasted_iota(jnp.int32, (tokens, tokens), 1)
    return gate & (cols <= rows)


def on_device(clean, delta, cotangent, w_query, w_key, w_value, masks):
    f32, bf16 = jnp.float32, jnp.bfloat16
    tok = clean.shape[0]
    feat = w_query.shape[1]
    half = feat // 2
    heads = half // DH
    rows_dev = w_query.shape[0]
    k = lax.axis_index("core")
    c = lax.axis_index("chip")
    chips = lax.axis_size("chip")
    first = k == 0

    x_in = (clean.astype(f32) + delta.astype(f32)).astype(bf16)
    x_pair = jnp.concatenate([x_in, swap(x_in)], axis=0)

    def cols(w, which):
        return lax.dynamic_slice_in_dim(w, which * half, half, axis=1)

    def chip_block(mats):
        mine = jnp.concatenate([cols(w, k) for w in mats], axis=1)
        recv = swap(jnp.concatenate([cols(w, 1 - k) for w in mats], axis=1))
        block = jnp.zeros((2 * rows_dev, mine.shape[1]), mine.dtype)
        block = lax.dynamic_update_slice_in_dim(block, mine, k * rows_dev, axis=0)
        return lax.dynamic_update_slice_in_dim(block, recv, (1 - k) * rows_dev, axis=0)

    span = 2 * rows_dev
    block = chip_block((w_query, w_key, w_value))
    parity = lax.axis_index("groups") % 2
    share = half
    width = 2 * half
    w_all = jnp.zeros((chips * span, width + share), bf16)
    for src, (ringed, swapped) in ring_gather(block, chips, c, parity):
        w_all = lax.dynamic_update_slice(w_all, ringed, (src * span, 0))
        w_all = lax.dynamic_update_slice(w_all, swapped, (src * span, width))
    at_q = parity * width
    at_k = (1 - parity) * share
    at_v = width - parity * share
    p_all = jnp.dot(x_pair, w_all, preferred_element_type=f32).astype(bf16)

    def pick(at):
        return lax.dynamic_slice_in_dim(p_all, at, share, axis=1).reshape(2, tok, heads, DH)

    query = pick(at_q)
    key = pick(at_k)
    value = pick(at_v)

    local = jnp.einsum("jthd,jthe->jhde", key, value, preferred_element_type=f32)
    state0, _ = exclusive_scan(local[0] + local[1], chips, False)
    state_mine = jnp.where(first, state0, state0 + local[1])
    state_other = jnp.where(first, state0 + local[0], state0)
    state_b = jnp.stack([state_mine, state_other]).astype(bf16)

    pair_masks = jnp.stack([masks[0], swap(masks[0])])
    allow = jax.vmap(dense_allow, in_axes=(0, None))(pair_masks, tok)

    scores = jnp.einsum("jthd,jshd->jhts", query, key, preferred_element_type=f32)
    attn = jnp.where(allow[:, None], scores, 0.0).astype(bf16)
    mixed = jnp.einsum("jhts,jshd->jthd", attn, value, preferred_element_type=f32)
    mixed = mixed + jnp.einsum("jthd,jhde->jthe", query, state_b, preferred_element_type=f32)
    root = jnp.sqrt(jnp.mean(mixed * mixed, axis=-1, keepdims=True) + EPSILON)
    normed = mixed / root

    out_b = normed.astype(bf16).reshape(2, tok, half)
    cot = cotangent.reshape(tok, 2, half)
    cot_mine = jnp.where(first, cot[:, 0], cot[:, 1])
    cot_other = jnp.where(first, cot[:, 1], cot[:, 0])
    grad_out = jnp.stack([cot_mine, swap(cot_other)]).astype(f32).reshape(2, tok, heads, DH)
    d_mixed = (grad_out - normed * jnp.mean(grad_out * normed, axis=-1, keepdims=True)) / root
    d_mixed_b = d_mixed.astype(bf16)
    grad_local = jnp.einsum("jthd,jthe->jhde", query, d_mixed_b, preferred_element_type=f32)

    d_scores = jnp.einsum("jthe,jshe->jhts", d_mixed_b, value, preferred_element_type=f32)
    d_attn = jnp.where(allow[:, None], d_scores, 0.0).astype(bf16)
    d_query = jnp.einsum("jhts,jshd->jthd", d_attn, key, preferred_element_type=f32)
    d_query = d_query + jnp.einsum("jthe,jhde->jthd", d_mixed_b, state_b, preferred_element_type=f32)
    dq_b = d_query.astype(bf16).reshape(2, tok, half)
    dims = (((1,), (1,)), ((), ()))
    w_qcols = lax.dynamic_slice_in_dim(w_all, at_q, share, axis=1)
    grad_q = [lax.dot_general(dq_b[j], w_qcols, dims, preferred_element_type=f32) for j in range(2)]
    later1, grad_q = exclusive_scan(grad_local[0] + grad_local[1], chips, True, grad_q)
    later_mine = jnp.where(first, later1 + grad_local[1], later1)
    later_other = jnp.where(first, later1, later1 + grad_local[0])
    later_b = jnp.stack([later_mine, later_other]).astype(bf16)
    out_send, later_b = lax.optimization_barrier((out_b[1], later_b))
    out_recv = swap(out_send)
    output = jnp.where(
        first,
        jnp.concatenate([out_b[0], out_recv], axis=1),
        jnp.concatenate([out_recv, out_b[0]], axis=1),
    )

    d_key = jnp.einsum("jhts,jthd->jshd", d_attn, query, preferred_element_type=f32)
    d_key = d_key + jnp.einsum("jshe,jhde->jshd", value, later_b, preferred_element_type=f32)
    d_value = jnp.einsum("jhts,jthe->jshe", attn, d_mixed_b, preferred_element_type=f32)
    d_value = d_value + jnp.einsum("jshd,jhde->jshe", key, later_b, preferred_element_type=f32)
    dk_b = d_key.astype(bf16).reshape(2, tok, half)
    dv_b = d_value.astype(bf16).reshape(2, tok, half)

    def grad_rows(j):
        g = grad_q[j]
        for d, at in ((dk_b[j], at_k), (dv_b[j], at_v)):
            w = lax.dynamic_slice_in_dim(w_all, at, share, axis=1)
            g = g + lax.dot_general(d, w, dims, preferred_element_type=f32)
        return g

    received = swap(grad_rows(1))
    own, received = lax.optimization_barrier((grad_rows(0), received))
    grad_input = (own + received).astype(bf16)
    return (output, grad_input)


def solution(mesh):
    groups = mesh.shape["groups"]
    seq = mesh.shape["seq"]
    devices = np.asarray(mesh.devices).reshape(groups, seq // 2, 2)
    inner = Mesh(devices, TOKENS)
    rows = P(TOKENS, None)
    weights = P(("chip", "core"), None)
    return jax.shard_map(
        on_device,
        mesh=inner,
        in_specs=(rows, rows, rows, weights, weights, weights, P(TOKENS, None, None)),
        out_specs=(rows, rows),
        check_vma=False,
    )
```

```python
import jax
import jax.numpy as jnp
import numpy as np
from jax import lax
from jax.sharding import Mesh
from jax.sharding import PartitionSpec as P

DH = 128
BLK = 128

EPSILON = 1e-06

TOKENS = ("groups", "chip", "core")


def swap(x):
    return lax.ppermute(x, "core", [(0, 1), (1, 0)])


def ring_order(chips):
    if chips % 2:
        return list(range(chips))
    return list(range(0, chips, 2)) + list(range(chips - 1, 0, -2))


def ring_gather(block, chips, c, p):
    order = ring_order(chips)
    place = np.zeros(chips, np.int32)
    place[np.asarray(order)] = np.arange(chips)
    order_t = jnp.asarray(order, jnp.int32)
    here = jnp.asarray(place)[c]
    ahead = [(order[p_], order[(p_ + 1) % chips]) for p_ in range(chips)]
    behind = [(order[p_], order[(p_ - 1) % chips]) for p_ in range(chips)]
    share = block.shape[1] // 3
    width = block.shape[1] - share
    groups = lax.axis_size("groups")
    partner = [(g, g ^ 1) for g in range(groups)]

    def land(piece):
        sent = lax.dynamic_slice_in_dim(piece, p * share, share, axis=1)
        return (piece, lax.ppermute(sent, "groups", partner))

    fwd = lax.dynamic_slice_in_dim(block, p * share, width, axis=1)
    got = [(c, (fwd, lax.dynamic_slice_in_dim(block, (1 - p) * width, share, axis=1)))]
    bwd = fwd
    for step in range(1, chips // 2 + 1):
        fwd = lax.ppermute(fwd, "chip", ahead)
        got.append((order_t[(here - step) % chips], land(fwd)))
        if step <= (chips - 1) // 2:
            bwd = lax.ppermute(bwd, "chip", behind)
            got.append((order_t[(here + step) % chips], land(bwd)))
    return got


def exclusive_scan(total, chips, reverse, side=()):
    incl = total
    excl = jnp.zeros_like(total)
    side = tuple(side)
    step = 0
    d = 1
    while d < chips:
        if reverse:
            perm = [(i, i - d) for i in range(d, chips)]
        else:
            perm = [(i, i + d) for i in range(chips - d)]
        got = lax.ppermute(incl, "chip", perm)
        if step < len(side):
            item, got = lax.optimization_barrier((side[step], got))
            side = side[:step] + (item,) + side[step + 1 :]
        step += 1
        incl = incl + got
        excl = excl + got
        d *= 2
    return excl, side


def dense_allow(block_masks, tokens):
    nb = tokens // BLK
    gate = jnp.broadcast_to((block_masks != 0)[:, None, :, None], (nb, BLK, nb, BLK)).reshape(tokens, tokens)
    rows = lax.broadcasted_iota(jnp.int32, (tokens, tokens), 0)
    cols = lax.broadcasted_iota(jnp.int32, (tokens, tokens), 1)
    return gate & (cols <= rows)


def on_device(clean, delta, cotangent, w_query, w_key, w_value, masks):
    f32, bf16 = jnp.float32, jnp.bfloat16
    tok = clean.shape[0]
    feat = w_query.shape[1]
    half = feat // 2
    heads = half // DH
    rows_dev = w_query.shape[0]
    k = lax.axis_index("core")
    c = lax.axis_index("chip")
    chips = lax.axis_size("chip")
    first = k == 0

    x_in = (clean.astype(f32) + delta.astype(f32)).astype(bf16)
    x_pair = jnp.concatenate([x_in, swap(x_in)], axis=0)

    def cols(w, which):
        return lax.dynamic_slice_in_dim(w, which * half, half, axis=1)

    def chip_block(mats):
        mine = jnp.concatenate([cols(w, k) for w in mats], axis=1)
        recv = swap(jnp.concatenate([cols(w, 1 - k) for w in mats], axis=1))
        block = jnp.zeros((2 * rows_dev, mine.shape[1]), mine.dtype)
        block = lax.dynamic_update_slice_in_dim(block, mine, k * rows_dev, axis=0)
        return lax.dynamic_update_slice_in_dim(block, recv, (1 - k) * rows_dev, axis=0)

    span = 2 * rows_dev
    block = chip_block((w_query, w_key, w_value))
    parity = lax.axis_index("groups") % 2
    share = half
    width = 2 * half
    w_all = jnp.zeros((chips * span, width + share), bf16)
    for src, (ringed, swapped) in ring_gather(block, chips, c, parity):
        w_all = lax.dynamic_update_slice(w_all, ringed, (src * span, 0))
        w_all = lax.dynamic_update_slice(w_all, swapped, (src * span, width))
    at_q = parity * width
    at_k = (1 - parity) * share
    at_v = width - parity * share
    p_all = jnp.dot(x_pair, w_all, preferred_element_type=f32).astype(bf16)

    def pick(at):
        return lax.dynamic_slice_in_dim(p_all, at, share, axis=1).reshape(2, tok, heads, DH)

    query = pick(at_q)
    key = pick(at_k)
    value = pick(at_v)

    local = jnp.einsum("jthd,jthe->jhde", key, value, preferred_element_type=f32)
    state0, _ = exclusive_scan(local[0] + local[1], chips, False)
    state_mine = jnp.where(first, state0, state0 + local[1])
    state_other = jnp.where(first, state0 + local[0], state0)
    state_b = jnp.stack([state_mine, state_other]).astype(bf16)

    pair_masks = jnp.stack([masks[0], swap(masks[0])])
    allow = jax.vmap(dense_allow, in_axes=(0, None))(pair_masks, tok)

    scores = jnp.einsum("jthd,jshd->jhts", query, key, preferred_element_type=f32)
    attn = jnp.where(allow[:, None], scores, 0.0).astype(bf16)
    mixed = jnp.einsum("jhts,jshd->jthd", attn, value, preferred_element_type=f32)
    mixed = mixed + jnp.einsum("jthd,jhde->jthe", query, state_b, preferred_element_type=f32)
    root = jnp.sqrt(jnp.mean(mixed * mixed, axis=-1, keepdims=True) + EPSILON)
    normed = mixed / root

    out_b = normed.astype(bf16).reshape(2, tok, half)
    cot = cotangent.reshape(tok, 2, half)
    cot_mine = jnp.where(first, cot[:, 0], cot[:, 1])
    cot_other = jnp.where(first, cot[:, 1], cot[:, 0])
    grad_out = jnp.stack([cot_mine, swap(cot_other)]).astype(f32).reshape(2, tok, heads, DH)
    d_mixed = (grad_out - normed * jnp.mean(grad_out * normed, axis=-1, keepdims=True)) / root
    d_mixed_b = d_mixed.astype(bf16)
    grad_local = jnp.einsum("jthd,jthe->jhde", query, d_mixed_b, preferred_element_type=f32)

    d_scores = jnp.einsum("jthe,jshe->jhts", d_mixed_b, value, preferred_element_type=f32)
    d_attn = jnp.where(allow[:, None], d_scores, 0.0).astype(bf16)
    d_query = jnp.einsum("jhts,jshd->jthd", d_attn, key, preferred_element_type=f32)
    d_query = d_query + jnp.einsum("jthe,jhde->jthd", d_mixed_b, state_b, preferred_element_type=f32)
    dq_b = d_query.astype(bf16).reshape(2, tok, half)
    dims = (((1,), (1,)), ((), ()))
    w_qcols = lax.dynamic_slice_in_dim(w_all, at_q, share, axis=1)
    grad_q = [lax.dot_general(dq_b[j], w_qcols, dims, preferred_element_type=f32) for j in range(2)]
    dk_intra = jnp.einsum("jhts,jthd->jshd", d_attn, query, preferred_element_type=f32)
    dv_intra = jnp.einsum("jhts,jthe->jshe", attn, d_mixed_b, preferred_element_type=f32)
    later1, (gq0, gq1, (dk_intra, dv_intra)) = exclusive_scan(
        grad_local[0] + grad_local[1], chips, True, (grad_q[0], grad_q[1], (dk_intra, dv_intra))
    )
    grad_q = [gq0, gq1]
    later_mine = jnp.where(first, later1 + grad_local[1], later1)
    later_other = jnp.where(first, later1, later1 + grad_local[0])
    later_b = jnp.stack([later_mine, later_other]).astype(bf16)
    out_send, later_b = lax.optimization_barrier((out_b[1], later_b))
    out_recv = swap(out_send)
    output = jnp.where(
        first,
        jnp.concatenate([out_b[0], out_recv], axis=1),
        jnp.concatenate([out_recv, out_b[0]], axis=1),
    )

    d_key = dk_intra + jnp.einsum("jshe,jhde->jshd", value, later_b, preferred_element_type=f32)
    d_value = dv_intra + jnp.einsum("jshd,jhde->jshe", key, later_b, preferred_element_type=f32)
    dk_b = d_key.astype(bf16).reshape(2, tok, half)
    dv_b = d_value.astype(bf16).reshape(2, tok, half)

    def grad_rows(j):
        g = grad_q[j]
        for d, at in ((dk_b[j], at_k), (dv_b[j], at_v)):
            w = lax.dynamic_slice_in_dim(w_all, at, share, axis=1)
            g = g + lax.dot_general(d, w, dims, preferred_element_type=f32)
        return g

    received = swap(grad_rows(1))
    own, received = lax.optimization_barrier((grad_rows(0), received))
    grad_input = (own + received).astype(bf16)
    return (output, grad_input)


def solution(mesh):
    groups = mesh.shape["groups"]
    seq = mesh.shape["seq"]
    devices = np.asarray(mesh.devices).reshape(groups, seq // 2, 2)
    inner = Mesh(devices, TOKENS)
    rows = P(TOKENS, None)
    weights = P(("chip", "core"), None)
    return jax.shard_map(
        on_device,
        mesh=inner,
        in_specs=(rows, rows, rows, weights, weights, weights, P(TOKENS, None, None)),
        out_specs=(rows, rows),
        check_vma=False,
    )
```

```python
import jax
import jax.numpy as jnp
import numpy as np
from jax import lax
from jax.sharding import Mesh
from jax.sharding import PartitionSpec as P

DH = 128
BLK = 128

EPSILON = 1e-06

TOKENS = ("groups", "chip", "core")


def swap(x):
    return lax.ppermute(x, "core", [(0, 1), (1, 0)])


def ring_order(chips):
    if chips % 2:
        return list(range(chips))
    return list(range(0, chips, 2)) + list(range(chips - 1, 0, -2))


def ring_gather(block, chips, c, p):
    order = ring_order(chips)
    place = np.zeros(chips, np.int32)
    place[np.asarray(order)] = np.arange(chips)
    order_t = jnp.asarray(order, jnp.int32)
    here = jnp.asarray(place)[c]
    ahead = [(order[p_], order[(p_ + 1) % chips]) for p_ in range(chips)]
    behind = [(order[p_], order[(p_ - 1) % chips]) for p_ in range(chips)]
    share = block.shape[1] // 3
    width = block.shape[1] - share
    groups = lax.axis_size("groups")
    partner = [(g, g ^ 1) for g in range(groups)]

    def land(piece):
        sent = lax.dynamic_slice_in_dim(piece, p * share, share, axis=1)
        return (piece, lax.ppermute(sent, "groups", partner))

    fwd = lax.dynamic_slice_in_dim(block, p * share, width, axis=1)
    got = [(c, (fwd, lax.dynamic_slice_in_dim(block, (1 - p) * width, share, axis=1)))]
    bwd = fwd
    for step in range(1, chips // 2 + 1):
        fwd = lax.ppermute(fwd, "chip", ahead)
        got.append((order_t[(here - step) % chips], land(fwd)))
        if step <= (chips - 1) // 2:
            bwd = lax.ppermute(bwd, "chip", behind)
            got.append((order_t[(here + step) % chips], land(bwd)))
    return got


def exclusive_scan(total, chips, reverse, side=()):
    incl = total
    excl = jnp.zeros_like(total)
    side = tuple(side)
    step = 0
    d = 1
    while d < chips:
        if reverse:
            perm = [(i, i - d) for i in range(d, chips)]
        else:
            perm = [(i, i + d) for i in range(chips - d)]
        got = lax.ppermute(incl, "chip", perm)
        if step < len(side):
            item, got = lax.optimization_barrier((side[step], got))
            side = side[:step] + (item,) + side[step + 1 :]
        step += 1
        incl = incl + got
        excl = excl + got
        d *= 2
    return excl, side


def dense_allow(block_masks, tokens):
    nb = tokens // BLK
    gate = jnp.broadcast_to((block_masks != 0)[:, None, :, None], (nb, BLK, nb, BLK)).reshape(tokens, tokens)
    rows = lax.broadcasted_iota(jnp.int32, (tokens, tokens), 0)
    cols = lax.broadcasted_iota(jnp.int32, (tokens, tokens), 1)
    return gate & (cols <= rows)


def on_device(clean, delta, cotangent, w_query, w_key, w_value, masks):
    f32, bf16 = jnp.float32, jnp.bfloat16
    tok = clean.shape[0]
    feat = w_query.shape[1]
    half = feat // 2
    heads = half // DH
    rows_dev = w_query.shape[0]
    k = lax.axis_index("core")
    c = lax.axis_index("chip")
    chips = lax.axis_size("chip")
    first = k == 0

    x_in = (clean.astype(f32) + delta.astype(f32)).astype(bf16)
    x_pair = jnp.concatenate([x_in, swap(x_in)], axis=0)

    def cols(w, which):
        return lax.dynamic_slice_in_dim(w, which * half, half, axis=1)

    def chip_block(mats):
        mine = jnp.concatenate([cols(w, k) for w in mats], axis=1)
        recv = swap(jnp.concatenate([cols(w, 1 - k) for w in mats], axis=1))
        block = jnp.zeros((2 * rows_dev, mine.shape[1]), mine.dtype)
        block = lax.dynamic_update_slice_in_dim(block, mine, k * rows_dev, axis=0)
        return lax.dynamic_update_slice_in_dim(block, recv, (1 - k) * rows_dev, axis=0)

    span = 2 * rows_dev
    block = chip_block((w_query, w_key, w_value))
    parity = lax.axis_index("groups") % 2
    share = half
    width = 2 * half
    w_all = jnp.zeros((chips * span, width + share), bf16)
    for src, (ringed, swapped) in ring_gather(block, chips, c, parity):
        w_all = lax.dynamic_update_slice(w_all, ringed, (src * span, 0))
        w_all = lax.dynamic_update_slice(w_all, swapped, (src * span, width))
    at_q = parity * width
    at_k = (1 - parity) * share
    at_v = width - parity * share
    w_kv = lax.dynamic_slice_in_dim(w_all, at_k, width, axis=1)
    p_kv = jnp.dot(x_pair, w_kv, preferred_element_type=f32).astype(bf16).reshape(2, tok, 2, heads, DH)
    key = p_kv[:, :, 0]
    value = p_kv[:, :, 1]
    w_qcols = lax.dynamic_slice_in_dim(w_all, at_q, share, axis=1)
    query = jnp.dot(x_pair, w_qcols, preferred_element_type=f32).astype(bf16).reshape(2, tok, heads, DH)

    local = jnp.einsum("jthd,jthe->jhde", key, value, preferred_element_type=f32)
    state0, _ = exclusive_scan(local[0] + local[1], chips, False)
    state_mine = jnp.where(first, state0, state0 + local[1])
    state_other = jnp.where(first, state0 + local[0], state0)
    state_b = jnp.stack([state_mine, state_other]).astype(bf16)

    pair_masks = jnp.stack([masks[0], swap(masks[0])])
    allow = jax.vmap(dense_allow, in_axes=(0, None))(pair_masks, tok)

    scores = jnp.einsum("jthd,jshd->jhts", query, key, preferred_element_type=f32)
    attn = jnp.where(allow[:, None], scores, 0.0).astype(bf16)
    mixed = jnp.einsum("jhts,jshd->jthd", attn, value, preferred_element_type=f32)
    mixed = mixed + jnp.einsum("jthd,jhde->jthe", query, state_b, preferred_element_type=f32)
    root = jnp.sqrt(jnp.mean(mixed * mixed, axis=-1, keepdims=True) + EPSILON)
    normed = mixed / root

    out_b = normed.astype(bf16).reshape(2, tok, half)
    cot = cotangent.reshape(tok, 2, half)
    cot_mine = jnp.where(first, cot[:, 0], cot[:, 1])
    cot_other = jnp.where(first, cot[:, 1], cot[:, 0])
    grad_out = jnp.stack([cot_mine, swap(cot_other)]).astype(f32).reshape(2, tok, heads, DH)
    d_mixed = (grad_out - normed * jnp.mean(grad_out * normed, axis=-1, keepdims=True)) / root
    d_mixed_b = d_mixed.astype(bf16)
    grad_local = jnp.einsum("jthd,jthe->jhde", query, d_mixed_b, preferred_element_type=f32)

    d_scores = jnp.einsum("jthe,jshe->jhts", d_mixed_b, value, preferred_element_type=f32)
    d_attn = jnp.where(allow[:, None], d_scores, 0.0).astype(bf16)
    d_query = jnp.einsum("jhts,jshd->jthd", d_attn, key, preferred_element_type=f32)
    d_query = d_query + jnp.einsum("jthe,jhde->jthd", d_mixed_b, state_b, preferred_element_type=f32)
    dq_b = d_query.astype(bf16).reshape(2, tok, half)
    dims = (((1,), (1,)), ((), ()))
    grad_q = [lax.dot_general(dq_b[j], w_qcols, dims, preferred_element_type=f32) for j in range(2)]
    dk_intra = jnp.einsum("jhts,jthd->jshd", d_attn, query, preferred_element_type=f32)
    dv_intra = jnp.einsum("jhts,jthe->jshe", attn, d_mixed_b, preferred_element_type=f32)
    later1, (gq0, gq1, (dk_intra, dv_intra)) = exclusive_scan(
        grad_local[0] + grad_local[1], chips, True, (grad_q[0], grad_q[1], (dk_intra, dv_intra))
    )
    grad_q = [gq0, gq1]
    later_mine = jnp.where(first, later1 + grad_local[1], later1)
    later_other = jnp.where(first, later1, later1 + grad_local[0])
    later_b = jnp.stack([later_mine, later_other]).astype(bf16)
    out_send, later_b = lax.optimization_barrier((out_b[1], later_b))
    out_recv = swap(out_send)
    output = jnp.where(
        first,
        jnp.concatenate([out_b[0], out_recv], axis=1),
        jnp.concatenate([out_recv, out_b[0]], axis=1),
    )

    d_key = dk_intra + jnp.einsum("jshe,jhde->jshd", value, later_b, preferred_element_type=f32)
    d_value = dv_intra + jnp.einsum("jshd,jhde->jshe", key, later_b, preferred_element_type=f32)
    dk_b = d_key.astype(bf16).reshape(2, tok, half)
    dv_b = d_value.astype(bf16).reshape(2, tok, half)

    def grad_rows(j):
        g = grad_q[j]
        for d, at in ((dk_b[j], at_k), (dv_b[j], at_v)):
            w = lax.dynamic_slice_in_dim(w_all, at, share, axis=1)
            g = g + lax.dot_general(d, w, dims, preferred_element_type=f32)
        return g

    received = swap(grad_rows(1))
    own, received = lax.optimization_barrier((grad_rows(0), received))
    grad_input = (own + received).astype(bf16)
    return (output, grad_input)


def solution(mesh):
    groups = mesh.shape["groups"]
    seq = mesh.shape["seq"]
    devices = np.asarray(mesh.devices).reshape(groups, seq // 2, 2)
    inner = Mesh(devices, TOKENS)
    rows = P(TOKENS, None)
    weights = P(("chip", "core"), None)
    return jax.shard_map(
        on_device,
        mesh=inner,
        in_specs=(rows, rows, rows, weights, weights, weights, P(TOKENS, None, None)),
        out_specs=(rows, rows),
        check_vma=False,
    )
```

```python
import jax
import jax.numpy as jnp
import numpy as np
from jax import lax
from jax.sharding import Mesh
from jax.sharding import PartitionSpec as P

DH = 128
BLK = 128

EPSILON = 1e-06

TOKENS = ("groups", "chip", "core")


def swap(x):
    return lax.ppermute(x, "core", [(0, 1), (1, 0)])


def ring_order(chips):
    if chips % 2:
        return list(range(chips))
    return list(range(0, chips, 2)) + list(range(chips - 1, 0, -2))


def ring_gather(block, chips, c, p):
    order = ring_order(chips)
    place = np.zeros(chips, np.int32)
    place[np.asarray(order)] = np.arange(chips)
    order_t = jnp.asarray(order, jnp.int32)
    here = jnp.asarray(place)[c]
    ahead = [(order[p_], order[(p_ + 1) % chips]) for p_ in range(chips)]
    behind = [(order[p_], order[(p_ - 1) % chips]) for p_ in range(chips)]
    share = block.shape[1] // 3
    width = block.shape[1] - share
    groups = lax.axis_size("groups")
    partner = [(g, g ^ 1) for g in range(groups)]

    def land(piece):
        sent = lax.dynamic_slice_in_dim(piece, p * share, share, axis=1)
        return (piece, lax.ppermute(sent, "groups", partner))

    fwd = lax.dynamic_slice_in_dim(block, p * share, width, axis=1)
    got = [(c, (fwd, lax.dynamic_slice_in_dim(block, (1 - p) * width, share, axis=1)))]
    bwd = fwd
    for step in range(1, chips // 2 + 1):
        fwd = lax.ppermute(fwd, "chip", ahead)
        got.append((order_t[(here - step) % chips], land(fwd)))
        if step <= (chips - 1) // 2:
            bwd = lax.ppermute(bwd, "chip", behind)
            got.append((order_t[(here + step) % chips], land(bwd)))
    return got


def exclusive_scan(total, chips, reverse, side=()):
    incl = total
    excl = jnp.zeros_like(total)
    side = tuple(side)
    step = 0
    d = 1
    while d < chips:
        if reverse:
            perm = [(i, i - d) for i in range(d, chips)]
        else:
            perm = [(i, i + d) for i in range(chips - d)]
        got = lax.ppermute(incl, "chip", perm)
        if step < len(side):
            item, got = lax.optimization_barrier((side[step], got))
            side = side[:step] + (item,) + side[step + 1 :]
        step += 1
        incl = incl + got
        excl = excl + got
        d *= 2
    return excl, side


def dense_allow(block_masks, tokens):
    nb = tokens // BLK
    gate = jnp.broadcast_to((block_masks != 0)[:, None, :, None], (nb, BLK, nb, BLK)).reshape(tokens, tokens)
    rows = lax.broadcasted_iota(jnp.int32, (tokens, tokens), 0)
    cols = lax.broadcasted_iota(jnp.int32, (tokens, tokens), 1)
    return gate & (cols <= rows)


def on_device(clean, delta, cotangent, w_query, w_key, w_value, masks):
    f32, bf16 = jnp.float32, jnp.bfloat16
    tok = clean.shape[0]
    feat = w_query.shape[1]
    half = feat // 2
    heads = half // DH
    rows_dev = w_query.shape[0]
    k = lax.axis_index("core")
    c = lax.axis_index("chip")
    chips = lax.axis_size("chip")
    first = k == 0

    x_in = (clean.astype(f32) + delta.astype(f32)).astype(bf16)
    x_pair = jnp.concatenate([x_in, swap(x_in)], axis=0)

    def cols(w, which):
        return lax.dynamic_slice_in_dim(w, which * half, half, axis=1)

    def chip_block(mats):
        mine = jnp.concatenate([cols(w, k) for w in mats], axis=1)
        recv = swap(jnp.concatenate([cols(w, 1 - k) for w in mats], axis=1))
        block = jnp.zeros((2 * rows_dev, mine.shape[1]), mine.dtype)
        block = lax.dynamic_update_slice_in_dim(block, mine, k * rows_dev, axis=0)
        return lax.dynamic_update_slice_in_dim(block, recv, (1 - k) * rows_dev, axis=0)

    span = 2 * rows_dev
    block = chip_block((w_query, w_key, w_value))
    parity = lax.axis_index("groups") % 2
    share = half
    width = 2 * half
    w_all = jnp.zeros((chips * span, width + share), bf16)
    for src, (ringed, swapped) in ring_gather(block, chips, c, parity):
        w_all = lax.dynamic_update_slice(w_all, ringed, (src * span, 0))
        w_all = lax.dynamic_update_slice(w_all, swapped, (src * span, width))
    at_q = parity * width
    at_k = (1 - parity) * share
    at_v = width - parity * share
    w_kv = lax.dynamic_slice_in_dim(w_all, at_k, width, axis=1)
    p_kv = jnp.dot(x_pair, w_kv, preferred_element_type=f32).astype(bf16).reshape(2, tok, 2, heads, DH)
    key = p_kv[:, :, 0]
    value = p_kv[:, :, 1]
    w_qcols = lax.dynamic_slice_in_dim(w_all, at_q, share, axis=1)
    query = jnp.dot(x_pair, w_qcols, preferred_element_type=f32).astype(bf16).reshape(2, tok, heads, DH)

    local = jnp.einsum("jthd,jthe->jhde", key, value, preferred_element_type=f32)
    pair_masks = jnp.stack([masks[0], swap(masks[0])])
    allow = jax.vmap(dense_allow, in_axes=(0, None))(pair_masks, tok)
    scores = jnp.einsum("jthd,jshd->jhts", query, key, preferred_element_type=f32)
    attn = jnp.where(allow[:, None], scores, 0.0).astype(bf16)
    intra = jnp.einsum("jhts,jshd->jthd", attn, value, preferred_element_type=f32)
    state0, (_, intra) = exclusive_scan(local[0] + local[1], chips, False, ((), intra))
    state_mine = jnp.where(first, state0, state0 + local[1])
    state_other = jnp.where(first, state0 + local[0], state0)
    state_b = jnp.stack([state_mine, state_other]).astype(bf16)


    mixed = intra + jnp.einsum("jthd,jhde->jthe", query, state_b, preferred_element_type=f32)
    root = jnp.sqrt(jnp.mean(mixed * mixed, axis=-1, keepdims=True) + EPSILON)
    normed = mixed / root

    out_b = normed.astype(bf16).reshape(2, tok, half)
    cot = cotangent.reshape(tok, 2, half)
    cot_mine = jnp.where(first, cot[:, 0], cot[:, 1])
    cot_other = jnp.where(first, cot[:, 1], cot[:, 0])
    grad_out = jnp.stack([cot_mine, swap(cot_other)]).astype(f32).reshape(2, tok, heads, DH)
    d_mixed = (grad_out - normed * jnp.mean(grad_out * normed, axis=-1, keepdims=True)) / root
    d_mixed_b = d_mixed.astype(bf16)
    grad_local = jnp.einsum("jthd,jthe->jhde", query, d_mixed_b, preferred_element_type=f32)

    d_scores = jnp.einsum("jthe,jshe->jhts", d_mixed_b, value, preferred_element_type=f32)
    d_attn = jnp.where(allow[:, None], d_scores, 0.0).astype(bf16)
    d_query = jnp.einsum("jhts,jshd->jthd", d_attn, key, preferred_element_type=f32)
    d_query = d_query + jnp.einsum("jthe,jhde->jthd", d_mixed_b, state_b, preferred_element_type=f32)
    dq_b = d_query.astype(bf16).reshape(2, tok, half)
    dims = (((1,), (1,)), ((), ()))
    grad_q = [lax.dot_general(dq_b[j], w_qcols, dims, preferred_element_type=f32) for j in range(2)]
    dk_intra = jnp.einsum("jhts,jthd->jshd", d_attn, query, preferred_element_type=f32)
    dv_intra = jnp.einsum("jhts,jthe->jshe", attn, d_mixed_b, preferred_element_type=f32)
    later1, (gq0, gq1, (dk_intra, dv_intra)) = exclusive_scan(
        grad_local[0] + grad_local[1], chips, True, (grad_q[0], grad_q[1], (dk_intra, dv_intra))
    )
    grad_q = [gq0, gq1]
    later_mine = jnp.where(first, later1 + grad_local[1], later1)
    later_other = jnp.where(first, later1, later1 + grad_local[0])
    later_b = jnp.stack([later_mine, later_other]).astype(bf16)
    out_send, later_b = lax.optimization_barrier((out_b[1], later_b))
    out_recv = swap(out_send)
    output = jnp.where(
        first,
        jnp.concatenate([out_b[0], out_recv], axis=1),
        jnp.concatenate([out_recv, out_b[0]], axis=1),
    )

    d_key = dk_intra + jnp.einsum("jshe,jhde->jshd", value, later_b, preferred_element_type=f32)
    d_value = dv_intra + jnp.einsum("jshd,jhde->jshe", key, later_b, preferred_element_type=f32)
    dk_b = d_key.astype(bf16).reshape(2, tok, half)
    dv_b = d_value.astype(bf16).reshape(2, tok, half)

    def grad_rows(j):
        g = grad_q[j]
        for d, at in ((dk_b[j], at_k), (dv_b[j], at_v)):
            w = lax.dynamic_slice_in_dim(w_all, at, share, axis=1)
            g = g + lax.dot_general(d, w, dims, preferred_element_type=f32)
        return g

    received = swap(grad_rows(1))
    own, received = lax.optimization_barrier((grad_rows(0), received))
    grad_input = (own + received).astype(bf16)
    return (output, grad_input)


def solution(mesh):
    groups = mesh.shape["groups"]
    seq = mesh.shape["seq"]
    devices = np.asarray(mesh.devices).reshape(groups, seq // 2, 2)
    inner = Mesh(devices, TOKENS)
    rows = P(TOKENS, None)
    weights = P(("chip", "core"), None)
    return jax.shard_map(
        on_device,
        mesh=inner,
        in_specs=(rows, rows, rows, weights, weights, weights, P(TOKENS, None, None)),
        out_specs=(rows, rows),
        check_vma=False,
    )
```

```python
import jax
import jax.numpy as jnp
import numpy as np
from jax import lax
from jax.sharding import Mesh
from jax.sharding import PartitionSpec as P

DH = 128
BLK = 128

EPSILON = 1e-06

TOKENS = ("groups", "chip", "core")


def swap(x):
    return lax.ppermute(x, "core", [(0, 1), (1, 0)])


def ring_order(chips):
    if chips % 2:
        return list(range(chips))
    return list(range(0, chips, 2)) + list(range(chips - 1, 0, -2))


def ring_gather(block, chips, c, p):
    order = ring_order(chips)
    place = np.zeros(chips, np.int32)
    place[np.asarray(order)] = np.arange(chips)
    order_t = jnp.asarray(order, jnp.int32)
    here = jnp.asarray(place)[c]
    ahead = [(order[p_], order[(p_ + 1) % chips]) for p_ in range(chips)]
    behind = [(order[p_], order[(p_ - 1) % chips]) for p_ in range(chips)]
    share = block.shape[1] // 3
    width = block.shape[1] - share
    groups = lax.axis_size("groups")
    partner = [(g, g ^ 1) for g in range(groups)]

    def land(piece):
        sent = lax.dynamic_slice_in_dim(piece, p * share, share, axis=1)
        return (piece, lax.ppermute(sent, "groups", partner))

    fwd = lax.dynamic_slice_in_dim(block, p * share, width, axis=1)
    got = [(c, (fwd, lax.dynamic_slice_in_dim(block, (1 - p) * width, share, axis=1)))]
    bwd = fwd
    for step in range(1, chips // 2 + 1):
        fwd = lax.ppermute(fwd, "chip", ahead)
        got.append((order_t[(here - step) % chips], land(fwd)))
        if step <= (chips - 1) // 2:
            bwd = lax.ppermute(bwd, "chip", behind)
            got.append((order_t[(here + step) % chips], land(bwd)))
    return got


def exclusive_scan(total, chips, reverse, side=()):
    incl = total
    excl = jnp.zeros_like(total)
    side = tuple(side)
    step = 0
    d = 1
    while d < chips:
        if reverse:
            perm = [(i, i - d) for i in range(d, chips)]
        else:
            perm = [(i, i + d) for i in range(chips - d)]
        got = lax.ppermute(incl, "chip", perm)
        if step < len(side):
            item, got = lax.optimization_barrier((side[step], got))
            side = side[:step] + (item,) + side[step + 1 :]
        step += 1
        incl = incl + got
        excl = excl + got
        d *= 2
    return excl, side


def dense_allow(block_masks, tokens):
    nb = tokens // BLK
    gate = jnp.broadcast_to((block_masks != 0)[:, None, :, None], (nb, BLK, nb, BLK)).reshape(tokens, tokens)
    rows = lax.broadcasted_iota(jnp.int32, (tokens, tokens), 0)
    cols = lax.broadcasted_iota(jnp.int32, (tokens, tokens), 1)
    return gate & (cols <= rows)


def on_device(clean, delta, cotangent, w_query, w_key, w_value, masks):
    f32, bf16 = jnp.float32, jnp.bfloat16
    tok = clean.shape[0]
    feat = w_query.shape[1]
    half = feat // 2
    heads = half // DH
    rows_dev = w_query.shape[0]
    k = lax.axis_index("core")
    c = lax.axis_index("chip")
    chips = lax.axis_size("chip")
    first = k == 0

    x_in = (clean.astype(f32) + delta.astype(f32)).astype(bf16)
    x_pair = jnp.concatenate([x_in, swap(x_in)], axis=0)

    def cols(w, which):
        return lax.dynamic_slice_in_dim(w, which * half, half, axis=1)

    def chip_block(mats):
        mine = jnp.concatenate([cols(w, k) for w in mats], axis=1)
        recv = swap(jnp.concatenate([cols(w, 1 - k) for w in mats], axis=1))
        block = jnp.zeros((2 * rows_dev, mine.shape[1]), mine.dtype)
        block = lax.dynamic_update_slice_in_dim(block, mine, k * rows_dev, axis=0)
        return lax.dynamic_update_slice_in_dim(block, recv, (1 - k) * rows_dev, axis=0)

    span = 2 * rows_dev
    block = chip_block((w_query, w_key, w_value))
    parity = lax.axis_index("groups") % 2
    share = half
    width = 2 * half
    w_all = jnp.zeros((chips * span, width + share), bf16)
    for src, (ringed, swapped) in ring_gather(block, chips, c, parity):
        w_all = lax.dynamic_update_slice(w_all, ringed, (src * span, 0))
        w_all = lax.dynamic_update_slice(w_all, swapped, (src * span, width))
    at_q = parity * width
    at_k = (1 - parity) * share
    at_v = width - parity * share
    w_kv = lax.dynamic_slice_in_dim(w_all, at_k, width, axis=1)
    p_kv = jnp.dot(x_pair, w_kv, preferred_element_type=f32).astype(bf16).reshape(2, tok, 2, heads, DH)
    key = p_kv[:, :, 0]
    value = p_kv[:, :, 1]
    w_qcols = lax.dynamic_slice_in_dim(w_all, at_q, share, axis=1)
    query = jnp.dot(x_pair, w_qcols, preferred_element_type=f32).astype(bf16).reshape(2, tok, heads, DH)

    local = jnp.einsum("jthd,jthe->jhde", key, value, preferred_element_type=f32)
    state0, _ = exclusive_scan(local[0] + local[1], chips, False)
    state_mine = jnp.where(first, state0, state0 + local[1])
    state_other = jnp.where(first, state0 + local[0], state0)
    state_b = jnp.stack([state_mine, state_other]).astype(bf16)

    pair_masks = jnp.stack([masks[0], swap(masks[0])])
    allow = jax.vmap(dense_allow, in_axes=(0, None))(pair_masks, tok)

    scores = jnp.einsum("jthd,jshd->jhts", query, key, preferred_element_type=f32)
    attn = jnp.where(allow[:, None], scores, 0.0).astype(bf16)
    mixed = jnp.einsum("jhts,jshd->jthd", attn, value, preferred_element_type=f32)
    mixed = mixed + jnp.einsum("jthd,jhde->jthe", query, state_b, preferred_element_type=f32)
    root = jnp.sqrt(jnp.mean(mixed * mixed, axis=-1, keepdims=True) + EPSILON)
    normed = mixed / root

    out_b = normed.astype(bf16).reshape(2, tok, half)
    cot = cotangent.reshape(tok, 2, half)
    cot_mine = jnp.where(first, cot[:, 0], cot[:, 1])
    cot_other = jnp.where(first, cot[:, 1], cot[:, 0])
    grad_out = jnp.stack([cot_mine, swap(cot_other)]).astype(f32).reshape(2, tok, heads, DH)
    d_mixed = (grad_out - normed * jnp.mean(grad_out * normed, axis=-1, keepdims=True)) / root
    d_mixed_b = d_mixed.astype(bf16)
    grad_local = jnp.einsum("jthd,jthe->jhde", query, d_mixed_b, preferred_element_type=f32)

    d_scores = jnp.einsum("jthe,jshe->jhts", d_mixed_b, value, preferred_element_type=f32)
    d_attn = jnp.where(allow[:, None], d_scores, 0.0).astype(bf16)
    d_query = jnp.einsum("jhts,jshd->jthd", d_attn, key, preferred_element_type=f32)
    d_query = d_query + jnp.einsum("jthe,jhde->jthd", d_mixed_b, state_b, preferred_element_type=f32)
    dq_b = d_query.astype(bf16).reshape(2, tok, half)
    dims = (((1,), (1,)), ((), ()))
    grad_q = [lax.dot_general(dq_b[j], w_qcols, dims, preferred_element_type=f32) for j in range(2)]
    dk_intra = jnp.einsum("jhts,jthd->jshd", d_attn, query, preferred_element_type=f32)
    dv_intra = jnp.einsum("jhts,jthe->jshe", attn, d_mixed_b, preferred_element_type=f32)
    later1, (gq0, gq1, (dk_intra, dv_intra)) = exclusive_scan(
        grad_local[0] + grad_local[1], chips, True, (grad_q[0], grad_q[1], (dk_intra, dv_intra))
    )
    grad_q = [gq0, gq1]
    later_mine = jnp.where(first, later1 + grad_local[1], later1)
    later_other = jnp.where(first, later1, later1 + grad_local[0])
    later_b = jnp.stack([later_mine, later_other]).astype(bf16)
    out_send, later_b = lax.optimization_barrier((out_b[1], later_b))
    out_recv = swap(out_send)
    output = jnp.where(
        first,
        jnp.concatenate([out_b[0], out_recv], axis=1),
        jnp.concatenate([out_recv, out_b[0]], axis=1),
    )

    d_key = dk_intra + jnp.einsum("jshe,jhde->jshd", value, later_b, preferred_element_type=f32)
    d_value = dv_intra + jnp.einsum("jshd,jhde->jshe", key, later_b, preferred_element_type=f32)
    dk_b = d_key.astype(bf16).reshape(2, tok, half)
    dv_b = d_value.astype(bf16).reshape(2, tok, half)

    def grad_rows(j, lo=0, hi=tok):
        g = grad_q[j][lo:hi]
        for d, at in ((dk_b[j], at_k), (dv_b[j], at_v)):
            w = lax.dynamic_slice_in_dim(w_all, at, share, axis=1)
            g = g + lax.dot_general(d[lo:hi], w, dims, preferred_element_type=f32)
        return g

    first_part = swap(grad_rows(1, 0, tok // 2))
    second_part = swap(grad_rows(1, tok // 2, tok))
    received = jnp.concatenate([first_part, second_part], axis=0)
    own, received = lax.optimization_barrier((grad_rows(0), received))
    grad_input = (own + received).astype(bf16)
    return (output, grad_input)


def solution(mesh):
    groups = mesh.shape["groups"]
    seq = mesh.shape["seq"]
    devices = np.asarray(mesh.devices).reshape(groups, seq // 2, 2)
    inner = Mesh(devices, TOKENS)
    rows = P(TOKENS, None)
    weights = P(("chip", "core"), None)
    return jax.shard_map(
        on_device,
        mesh=inner,
        in_specs=(rows, rows, rows, weights, weights, weights, P(TOKENS, None, None)),
        out_specs=(rows, rows),
        check_vma=False,
    )
```

```python
import jax
import jax.numpy as jnp
import numpy as np
from jax import lax
from jax.sharding import Mesh
from jax.sharding import PartitionSpec as P

DH = 128
BLK = 128

EPSILON = 1e-06

TOKENS = ("groups", "chip", "core")


def swap(x):
    return lax.ppermute(x, "core", [(0, 1), (1, 0)])


def ring_order(chips):
    if chips % 2:
        return list(range(chips))
    return list(range(0, chips, 2)) + list(range(chips - 1, 0, -2))


def ring_gather(block, chips, c, p):
    order = ring_order(chips)
    place = np.zeros(chips, np.int32)
    place[np.asarray(order)] = np.arange(chips)
    order_t = jnp.asarray(order, jnp.int32)
    here = jnp.asarray(place)[c]
    ahead = [(order[p_], order[(p_ + 1) % chips]) for p_ in range(chips)]
    behind = [(order[p_], order[(p_ - 1) % chips]) for p_ in range(chips)]
    share = block.shape[1] // 3
    width = block.shape[1] - share
    groups = lax.axis_size("groups")
    partner = [(g, g ^ 1) for g in range(groups)]

    def land(piece):
        sent = lax.dynamic_slice_in_dim(piece, p * share, share, axis=1)
        return (piece, lax.ppermute(sent, "groups", partner))

    fwd = lax.dynamic_slice_in_dim(block, p * share, width, axis=1)
    got = [(c, (fwd, lax.dynamic_slice_in_dim(block, (1 - p) * width, share, axis=1)))]
    bwd = fwd
    for step in range(1, chips // 2 + 1):
        fwd = lax.ppermute(fwd, "chip", ahead)
        got.append((order_t[(here - step) % chips], land(fwd)))
        if step <= (chips - 1) // 2:
            bwd = lax.ppermute(bwd, "chip", behind)
            got.append((order_t[(here + step) % chips], land(bwd)))
    return got


def exclusive_scan(total, chips, reverse, side=()):
    incl = total
    excl = jnp.zeros_like(total)
    side = tuple(side)
    step = 0
    d = 1
    while d < chips:
        if reverse:
            perm = [(i, i - d) for i in range(d, chips)]
        else:
            perm = [(i, i + d) for i in range(chips - d)]
        got = lax.ppermute(incl, "chip", perm)
        if step < len(side):
            item, got = lax.optimization_barrier((side[step], got))
            side = side[:step] + (item,) + side[step + 1 :]
        step += 1
        incl = incl + got
        excl = excl + got
        d *= 2
    return excl, side


def dense_allow(block_masks, tokens):
    nb = tokens // BLK
    gate = jnp.broadcast_to((block_masks != 0)[:, None, :, None], (nb, BLK, nb, BLK)).reshape(tokens, tokens)
    rows = lax.broadcasted_iota(jnp.int32, (tokens, tokens), 0)
    cols = lax.broadcasted_iota(jnp.int32, (tokens, tokens), 1)
    return gate & (cols <= rows)


def on_device(clean, delta, cotangent, w_query, w_key, w_value, masks):
    f32, bf16 = jnp.float32, jnp.bfloat16
    tok = clean.shape[0]
    feat = w_query.shape[1]
    half = feat // 2
    heads = half // DH
    rows_dev = w_query.shape[0]
    k = lax.axis_index("core")
    c = lax.axis_index("chip")
    chips = lax.axis_size("chip")
    first = k == 0

    x_in = (clean.astype(f32) + delta.astype(f32)).astype(bf16)
    x_pair = jnp.concatenate([x_in, swap(x_in)], axis=0)

    def cols(w, which):
        return lax.dynamic_slice_in_dim(w, which * half, half, axis=1)

    def chip_block(mats):
        mine = jnp.concatenate([cols(w, k) for w in mats], axis=1)
        recv = swap(jnp.concatenate([cols(w, 1 - k) for w in mats], axis=1))
        block = jnp.zeros((2 * rows_dev, mine.shape[1]), mine.dtype)
        block = lax.dynamic_update_slice_in_dim(block, mine, k * rows_dev, axis=0)
        return lax.dynamic_update_slice_in_dim(block, recv, (1 - k) * rows_dev, axis=0)

    span = 2 * rows_dev
    block = chip_block((w_query, w_key, w_value))
    parity = lax.axis_index("groups") % 2
    share = half
    width = 2 * half
    w_all = jnp.zeros((chips * span, width + share), bf16)
    for src, (ringed, swapped) in ring_gather(block, chips, c, parity):
        w_all = lax.dynamic_update_slice(w_all, ringed, (src * span, 0))
        w_all = lax.dynamic_update_slice(w_all, swapped, (src * span, width))
    at_q = parity * width
    at_k = (1 - parity) * share
    at_v = width - parity * share
    w_kv = lax.dynamic_slice_in_dim(w_all, at_k, width, axis=1)
    p_kv = jnp.dot(x_pair, w_kv, preferred_element_type=f32).astype(bf16).reshape(2, tok, 2, heads, DH)
    key = p_kv[:, :, 0]
    value = p_kv[:, :, 1]
    w_qcols = lax.dynamic_slice_in_dim(w_all, at_q, share, axis=1)
    query = jnp.dot(x_pair, w_qcols, preferred_element_type=f32).astype(bf16).reshape(2, tok, heads, DH)

    local = jnp.einsum("jthd,jthe->jhde", key, value, preferred_element_type=f32)
    state0, _ = exclusive_scan(local[0] + local[1], chips, False)
    state_mine = jnp.where(first, state0, state0 + local[1])
    state_other = jnp.where(first, state0 + local[0], state0)
    state_b = jnp.stack([state_mine, state_other]).astype(bf16)

    pair_masks = jnp.stack([masks[0], swap(masks[0])])
    allow = jax.vmap(dense_allow, in_axes=(0, None))(pair_masks, tok)

    scores = jnp.einsum("jthd,jshd->jhts", query, key, preferred_element_type=f32)
    attn = jnp.where(allow[:, None], scores, 0.0).astype(bf16)
    mixed = jnp.einsum("jhts,jshd->jthd", attn, value, preferred_element_type=f32)
    mixed = mixed + jnp.einsum("jthd,jhde->jthe", query, state_b, preferred_element_type=f32)
    root = jnp.sqrt(jnp.mean(mixed * mixed, axis=-1, keepdims=True) + EPSILON)
    normed = mixed / root

    out_b = normed.astype(bf16).reshape(2, tok, half)
    cot = cotangent.reshape(tok, 2, half)
    cot_mine = jnp.where(first, cot[:, 0], cot[:, 1])
    cot_other = jnp.where(first, cot[:, 1], cot[:, 0])
    grad_out = jnp.stack([cot_mine, swap(cot_other)]).astype(f32).reshape(2, tok, heads, DH)
    d_mixed = (grad_out - normed * jnp.mean(grad_out * normed, axis=-1, keepdims=True)) / root
    d_mixed_b = d_mixed.astype(bf16)
    grad_local = jnp.einsum("jthd,jthe->jhde", query, d_mixed_b, preferred_element_type=f32)

    d_scores = jnp.einsum("jthe,jshe->jhts", d_mixed_b, value, preferred_element_type=f32)
    d_attn = jnp.where(allow[:, None], d_scores, 0.0).astype(bf16)
    d_query = jnp.einsum("jhts,jshd->jthd", d_attn, key, preferred_element_type=f32)
    d_query = d_query + jnp.einsum("jthe,jhde->jthd", d_mixed_b, state_b, preferred_element_type=f32)
    dq_b = d_query.astype(bf16).reshape(2, tok, half)
    dims = (((1,), (1,)), ((), ()))
    grad_q = [lax.dot_general(dq_b[j], w_qcols, dims, preferred_element_type=f32) for j in range(2)]
    dk_intra = jnp.einsum("jhts,jthd->jshd", d_attn, query, preferred_element_type=f32)
    dv_intra = jnp.einsum("jhts,jthe->jshe", attn, d_mixed_b, preferred_element_type=f32)
    later1, (gq0, gq1, (dk_intra, dv_intra)) = exclusive_scan(
        grad_local[0] + grad_local[1], chips, True, (grad_q[0], grad_q[1], (dk_intra, dv_intra))
    )
    grad_q = [gq0, gq1]
    later_mine = jnp.where(first, later1 + grad_local[1], later1)
    later_other = jnp.where(first, later1, later1 + grad_local[0])
    later_b = jnp.stack([later_mine, later_other]).astype(bf16)
    out_send, later_b = lax.optimization_barrier((out_b[1], later_b))
    out_recv = swap(out_send)
    output = jnp.zeros((tok, feat), bf16)
    output = lax.dynamic_update_slice_in_dim(output, out_b[0], k * half, axis=1)
    output = lax.dynamic_update_slice_in_dim(output, out_recv, (1 - k) * half, axis=1)

    d_key = dk_intra + jnp.einsum("jshe,jhde->jshd", value, later_b, preferred_element_type=f32)
    d_value = dv_intra + jnp.einsum("jshd,jhde->jshe", key, later_b, preferred_element_type=f32)
    dk_b = d_key.astype(bf16).reshape(2, tok, half)
    dv_b = d_value.astype(bf16).reshape(2, tok, half)

    def grad_rows(j):
        g = grad_q[j]
        for d, at in ((dk_b[j], at_k), (dv_b[j], at_v)):
            w = lax.dynamic_slice_in_dim(w_all, at, share, axis=1)
            g = g + lax.dot_general(d, w, dims, preferred_element_type=f32)
        return g

    received = swap(grad_rows(1))
    own, received = lax.optimization_barrier((grad_rows(0), received))
    grad_input = (own + received).astype(bf16)
    return (output, grad_input)


def solution(mesh):
    groups = mesh.shape["groups"]
    seq = mesh.shape["seq"]
    devices = np.asarray(mesh.devices).reshape(groups, seq // 2, 2)
    inner = Mesh(devices, TOKENS)
    rows = P(TOKENS, None)
    weights = P(("chip", "core"), None)
    return jax.shard_map(
        on_device,
        mesh=inner,
        in_specs=(rows, rows, rows, weights, weights, weights, P(TOKENS, None, None)),
        out_specs=(rows, rows),
        check_vma=False,
    )
```
